32 devices in a mesh: left: 4 (over y, x), right: 8 (over z, core).
Axes of the slice: x: 2, y: 2, z: 4, core: 2. Of those that a mesh axis runs over, the one named last changes fastest.
Arguments:
- state: float32 [32, 1024, 1024], P(('left', 'right')), may hold values from -20 to 20
- left_env: bfloat16 [2, 32, 1024, 1024], P(None, ('left', 'right')), may hold values from -0.5 to 2.5
- right_env: bfloat16 [2, 32, 1024, 1024], P(None, ('left', 'right')), may hold values from -0.5 to 2.5
- site_ops: float32 [2, 4, 4], replicated, may hold values from -3 to 3
- left_live: int32 [8], replicated, may hold values from 1 to 4
- right_live: int32 [10], replicated, may hold values from 1 to 4
Outputs:
- next_vector: float32 [32, 1024, 1024], P(('left', 'right'))
- coefficients: float32 [2], replicated
The draws below stay inside these ranges and needn't reach their ends.
All inputs are finite; a program needn't handle non-finite values.
Results may differ from the reference program's by a relative error of at most 0.0047.
Values may be sent and summed in bfloat16 or wider, within the bound.
No kernel may reach another device: no remote copies, remote signals or barrier semaphores. Data moves between devices by JAX's collectives and lax.ppermute only.
A program may use at most 64 MiB of HBM per device.

```python
import jax
import jax.numpy as jnp
from jax import lax

BLOCK = 256
SEC_BLOCKS = 4
PAIR = 4
SEC = 1024
SECTORS = 8
RSECTORS = 10
BLOCKS = 32


def env_blocks(key, count):
    rows = jnp.arange(SEC, dtype=jnp.int32)
    identity = (rows[:, None] == rows[None, :]).astype(jnp.float32)
    spread = jnp.clip(jax.random.normal(key, (2, count, SEC, SEC), jnp.float32), -6.0, 6.0)
    diagonal = jax.random.uniform(jax.random.fold_in(key, 1), (2, count, 1, SEC), jnp.float32, 0.5, 1.5)
    return spread * (0.6 / SEC ** 0.5) + identity * diagonal


def draw_left_env(key, part):
    base = env_blocks(jax.random.fold_in(key, 5), SECTORS)
    return jnp.repeat(base, PAIR, axis=1).astype(jnp.bfloat16)


def draw_right_env(key, part):
    base = env_blocks(jax.random.fold_in(key, 7), SECTORS + 2)
    block_ids = jnp.arange(BLOCKS, dtype=jnp.int32)
    index = (block_ids // PAIR + (block_ids % PAIR + 1) // 2).astype(jnp.int32)
    return jnp.take(base, index, axis=1).astype(jnp.bfloat16)


def draw_state(key, part):
    place = jnp.arange(BLOCKS, dtype=jnp.float32) / BLOCKS
    ramp = jnp.exp(0.6 * place)[:, None, None]
    values = jnp.clip(jax.random.normal(key, (BLOCKS, SEC, SEC), jnp.float32), -6.0, 6.0)
    return (values * ramp).astype(jnp.float32)


def touch_ends(result, own_key, low, high):
    longest = result.shape.index(max(result.shape))
    spots = []
    for shift in (0, 1):
        where = [jax.random.randint(jax.random.fold_in(own_key, axis), (), 0, length) for axis, length in enumerate(result.shape)]
        where[longest] = (where[longest] + shift) % result.shape[longest]
        spots.append(tuple(where))
    return result.at[spots[0]].set(low).at[spots[1]].set(high)


def scatter_about(stream_key, extent, scale, bound, held_as=jnp.bfloat16):
    values = jax.random.normal(stream_key, extent, jnp.float32) * scale
    return jnp.minimum(jnp.maximum(values, -bound), bound).astype(held_as)


def setup_inputs(seed: int = 0) -> dict:
    streams_of = jax.random.split(jax.random.key(seed), 7)
    state = draw_state(jax.random.fold_in(streams_of[6], 71), 0)
    left_env = draw_left_env(jax.random.fold_in(streams_of[6], 71), 0)
    right_env = draw_right_env(jax.random.fold_in(streams_of[6], 71), 0)
    site_ops = scatter_about(streams_of[3], (2, PAIR, PAIR), PAIR ** -0.5, 3.0, jnp.float32)
    left_live = touch_ends(jax.random.randint(streams_of[4], (SECTORS,), 1, SEC_BLOCKS + 1), jax.random.fold_in(streams_of[4], 1), 1, SEC_BLOCKS).astype(jnp.int32)
    right_live = touch_ends(jax.random.randint(streams_of[5], (RSECTORS,), 1, SEC_BLOCKS + 1), jax.random.fold_in(streams_of[5], 1), 1, SEC_BLOCKS).astype(jnp.int32)
    return {"state": state, "left_env": left_env, "right_env": right_env, "site_ops": site_ops, "left_live": left_live, "right_live": right_live}


def pair_steps():
    return ((jnp.arange(PAIR, dtype=jnp.int32) + 1) // 2).astype(jnp.int32)

def source_weight(site_ops, target, offset):
    own_pair = (target % PAIR).astype(jnp.int32)
    source_pair = ((own_pair - offset) % PAIR).astype(jnp.int32)
    valid = target >= offset
    return jnp.where(valid, site_ops[0, own_pair, source_pair], jnp.zeros((), site_ops.dtype))

def reference(state, left_env, right_env, site_ops, left_live, right_live):
    steps = pair_steps()
    block_ids = jnp.arange(BLOCKS, dtype=jnp.int32)
    sectors = (block_ids // PAIR).astype(jnp.int32)
    pair_of = (block_ids % PAIR).astype(jnp.int32)
    row_live = left_live[sectors] * BLOCK
    col_live = right_live[sectors + steps[pair_of]] * BLOCK
    positions = jnp.arange(SEC, dtype=jnp.int32)
    row_mask = (positions[None, :] < row_live[:, None]).astype(jnp.float32)
    col_mask = (positions[None, :] < col_live[:, None]).astype(jnp.float32)
    entries = float(BLOCKS * SEC * SEC)
    masked = state * row_mask[:, :, None] * col_mask[:, None, :]
    vector = masked / jnp.sqrt(jnp.sum(masked * masked) / entries + 1e-06)
    rounded = vector.astype(jnp.bfloat16)

    def one_block(target):
        own = lax.dynamic_index_in_dim(rounded, target, 0, keepdims=False)
        two = lax.dynamic_index_in_dim(rounded, jnp.maximum(target - 2, 0).astype(jnp.int32), 0, keepdims=False)
        three = lax.dynamic_index_in_dim(rounded, jnp.maximum(target - 3, 0).astype(jnp.int32), 0, keepdims=False)
        weight_two = source_weight(site_ops, target, 2)
        weight_three = source_weight(site_ops, target, 3)
        source = (weight_two * two.astype(jnp.float32) + weight_three * three.astype(jnp.float32)).astype(jnp.bfloat16)
        right_zero = lax.dynamic_index_in_dim(right_env[0], target, 0, keepdims=False)
        right_one = lax.dynamic_index_in_dim(right_env[1], target, 0, keepdims=False)
        left_zero = lax.dynamic_index_in_dim(left_env[0], target, 0, keepdims=False)
        left_one = lax.dynamic_index_in_dim(left_env[1], target, 0, keepdims=False)
        part_zero = jnp.dot(source, right_zero, preferred_element_type=jnp.float32).astype(jnp.bfloat16)
        part_one = jnp.dot(own, right_one, preferred_element_type=jnp.float32).astype(jnp.bfloat16)
        own_pair = (target % PAIR).astype(jnp.int32)
        diag_weight = site_ops[1, own_pair, own_pair]
        image = jnp.dot(left_zero, part_zero, preferred_element_type=jnp.float32)
        image = image + diag_weight * jnp.dot(left_one, part_one, preferred_element_type=jnp.float32)
        rows = lax.dynamic_index_in_dim(row_mask, target, 0, keepdims=False)
        cols = lax.dynamic_index_in_dim(col_mask, target, 0, keepdims=False)
        return image * rows[:, None] * cols[None, :]
    image = lax.map(one_block, block_ids)
    alpha_value = jnp.sum(vector * image) / entries
    residual = image - alpha_value * vector
    beta_value = jnp.sqrt(jnp.sum(residual * residual) / entries + 1e-06)
    return (residual / beta_value, jnp.stack([alpha_value, beta_value]).astype(jnp.float32))
```

```python
import jax
import jax.numpy as jnp
from jax import lax
from jax.sharding import PartitionSpec as P

BLOCK = 256
AXES = ("left", "right")
CHUNKS = 4


def shift_up(block, distance):
    devices = range(lax.axis_size(AXES))
    route = [(i - distance, i) for i in devices if i - distance in devices]
    return lax.ppermute(block, AXES, route)


def butterfly_sum(values):
    count = lax.axis_size(AXES)
    bit = 1
    while bit < count:
        route = [(i, i ^ bit) for i in range(count) if (i ^ bit) < count]
        values = values + lax.ppermute(values, AXES, route)
        bit *= 2
    return values


def small_lookup(table, index):
    places = jnp.arange(table.shape[0], dtype=jnp.int32)
    return jnp.sum(jnp.where(places == index, table, jnp.zeros_like(table)))


def table_entry(table, row, column):
    rows = jnp.arange(table.shape[0], dtype=jnp.int32)[:, None]
    columns = jnp.arange(table.shape[1], dtype=jnp.int32)[None, :]
    return jnp.sum(jnp.where((rows == row) & (columns == column), table, jnp.zeros_like(table)))


def per_device(state, left_env, right_env, site_ops, left_live, right_live):
    pairs = site_ops.shape[1]
    sec_size = state.shape[1]
    block_index = lax.axis_index("left") * lax.axis_size("right") + lax.axis_index("right")
    own_pair = block_index % pairs
    sector = block_index // pairs
    steps = (jnp.arange(pairs, dtype=jnp.int32) + 1) // 2
    own_step = small_lookup(steps, own_pair)
    positions = jnp.arange(sec_size, dtype=jnp.int32)
    row_mask = (positions < small_lookup(left_live, sector) * BLOCK).astype(jnp.float32)
    col_mask = (positions < small_lookup(right_live, sector + own_step) * BLOCK).astype(jnp.float32)
    live = row_mask[:, None] * col_mask[None, :]
    entries = float(state.shape[0] * sec_size * sec_size * lax.axis_size(AXES))

    masked = state[0] * live
    start_sum = butterfly_sum(jnp.sum(masked * masked))
    start_mean = start_sum / entries
    vector = masked / jnp.sqrt(start_mean + 1e-06)
    rounded = vector.astype(jnp.bfloat16)

    weights = []
    for offset in (2, 3):
        source_pair = (own_pair - offset) % pairs
        valid = block_index >= offset
        weights.append(
            jnp.where(
                valid, table_entry(site_ops[0], own_pair, source_pair), jnp.zeros((), jnp.float32)
            )
        )

    part_one = jnp.dot(rounded, right_env[1, 0], preferred_element_type=jnp.float32).astype(
        jnp.bfloat16
    )
    diag_weight = table_entry(site_ops[1], own_pair, own_pair)
    image = diag_weight * jnp.dot(left_env[1, 0], part_one, preferred_element_type=jnp.float32)

    rows = sec_size // CHUNKS
    for c in range(CHUNKS):
        piece = rounded[c * rows:(c + 1) * rows]
        far_two = shift_up(piece, 2)
        far_three = shift_up(far_two, 1)
        source = (
            weights[0] * far_two.astype(jnp.float32) + weights[1] * far_three.astype(jnp.float32)
        ).astype(jnp.bfloat16)
        part_zero = jnp.dot(source, right_env[0, 0], preferred_element_type=jnp.float32).astype(
            jnp.bfloat16
        )
        image = image + jnp.dot(
            left_env[0, 0][:, c * rows:(c + 1) * rows], part_zero, preferred_element_type=jnp.float32
        )
    image = image * live

    sums = butterfly_sum(jnp.stack([jnp.sum(vector * image), jnp.sum(image * image)]))
    alpha_value = sums[0] / entries
    vector_mean = start_mean / (start_mean + 1e-06)
    residual_mean = sums[1] / entries - alpha_value * alpha_value * (2.0 - vector_mean)
    residual = image - alpha_value * vector
    beta_value = jnp.sqrt(residual_mean + 1e-06)
    next_vector = residual / beta_value
    return (next_vector[None], jnp.stack([alpha_value, beta_value]))


def solution(mesh):
    in_specs = (
        P(AXES, None, None),
        P(None, AXES, None, None),
        P(None, AXES, None, None),
        P(),
        P(),
        P(),
    )
    out_specs = (P(AXES, None, None), P())
    return jax.shard_map(
        per_device, mesh=mesh, in_specs=in_specs, out_specs=out_specs, check_vma=False
    )
```

```python
import jax
import jax.numpy as jnp
from jax import lax
from jax.sharding import PartitionSpec as P
from jax.experimental.layout import Layout, with_layout_constraint

BLOCK = 256
AXES = ("left", "right")
CHUNKS = 4


def shift_up(block, distance):
    devices = range(lax.axis_size(AXES))
    route = [(i - distance, i) for i in devices if i - distance in devices]
    return lax.ppermute(block, AXES, route)


def butterfly_sum(values):
    count = lax.axis_size(AXES)
    bit = 1
    while bit < count:
        route = [(i, i ^ bit) for i in range(count) if (i ^ bit) < count]
        values = values + lax.ppermute(values, AXES, route)
        bit *= 2
    return values


def row_major(array):
    return with_layout_constraint(array, Layout(major_to_minor=tuple(range(array.ndim))))


def small_lookup(table, index):
    places = jnp.arange(table.shape[0], dtype=jnp.int32)
    return jnp.sum(jnp.where(places == index, table, jnp.zeros_like(table)))


def table_entry(table, row, column):
    rows = jnp.arange(table.shape[0], dtype=jnp.int32)[:, None]
    columns = jnp.arange(table.shape[1], dtype=jnp.int32)[None, :]
    return jnp.sum(jnp.where((rows == row) & (columns == column), table, jnp.zeros_like(table)))


def per_device(state, left_env, right_env, site_ops, left_live, right_live):
    pairs = site_ops.shape[1]
    sec_size = state.shape[1]
    block_index = lax.axis_index("left") * lax.axis_size("right") + lax.axis_index("right")
    own_pair = block_index % pairs
    sector = block_index // pairs
    steps = (jnp.arange(pairs, dtype=jnp.int32) + 1) // 2
    own_step = small_lookup(steps, own_pair)
    positions = jnp.arange(sec_size, dtype=jnp.int32)
    row_mask = (positions < small_lookup(left_live, sector) * BLOCK).astype(jnp.float32)
    col_mask = (positions < small_lookup(right_live, sector + own_step) * BLOCK).astype(jnp.float32)
    live = row_mask[:, None] * col_mask[None, :]
    entries = float(state.shape[0] * sec_size * sec_size * lax.axis_size(AXES))

    masked = state[0] * live
    start_sum = butterfly_sum(jnp.sum(masked * masked))
    start_mean = start_sum / entries
    vector = masked / jnp.sqrt(start_mean + 1e-06)
    rounded = row_major(vector.astype(jnp.bfloat16))

    weights = []
    for offset in (2, 3):
        source_pair = (own_pair - offset) % pairs
        valid = block_index >= offset
        weights.append(
            jnp.where(
                valid, table_entry(site_ops[0], own_pair, source_pair), jnp.zeros((), jnp.float32)
            )
        )

    part_one = jnp.dot(rounded, right_env[1, 0], preferred_element_type=jnp.float32).astype(
        jnp.bfloat16
    )
    diag_weight = table_entry(site_ops[1], own_pair, own_pair)
    image_one = diag_weight * jnp.dot(left_env[1, 0], part_one, preferred_element_type=jnp.float32)

    rows = sec_size // CHUNKS
    pieces = [rounded[c * rows:(c + 1) * rows] for c in range(CHUNKS)]
    image_one, pieces[-1] = lax.optimization_barrier((image_one, pieces[-1]))
    image = image_one
    for c in range(CHUNKS):
        far_two = shift_up(pieces[c], 2)
        far_three = shift_up(far_two, 1)
        source = (
            weights[0] * far_two.astype(jnp.float32) + weights[1] * far_three.astype(jnp.float32)
        ).astype(jnp.bfloat16)
        part_zero = jnp.dot(source, right_env[0, 0], preferred_element_type=jnp.float32).astype(
            jnp.bfloat16
        )
        image = image + jnp.dot(
            left_env[0, 0][:, c * rows:(c + 1) * rows], part_zero, preferred_element_type=jnp.float32
        )
    image = row_major(image * live)

    sums = butterfly_sum(jnp.stack([jnp.sum(vector * image), jnp.sum(image * image)]))
    alpha_value = sums[0] / entries
    vector_mean = start_mean / (start_mean + 1e-06)
    residual_mean = sums[1] / entries - alpha_value * alpha_value * (2.0 - vector_mean)
    residual = image - alpha_value * vector
    beta_value = jnp.sqrt(residual_mean + 1e-06)
    next_vector = residual / beta_value
    return (next_vector[None], jnp.stack([alpha_value, beta_value]))


def solution(mesh):
    in_specs = (
        P(AXES, None, None),
        P(None, AXES, None, None),
        P(None, AXES, None, None),
        P(),
        P(),
        P(),
    )
    out_specs = (P(AXES, None, None), P())
    return jax.shard_map(
        per_device, mesh=mesh, in_specs=in_specs, out_specs=out_specs, check_vma=False
    )
```

```python
import jax
import jax.numpy as jnp
from jax import lax
from jax.sharding import PartitionSpec as P
from jax.experimental.layout import Layout, with_layout_constraint

BLOCK = 256
AXES = ("left", "right")
CHUNKS = 4


def shift_up(block, distance):
    devices = range(lax.axis_size(AXES))
    route = [(i - distance, i) for i in devices if i - distance in devices]
    return lax.ppermute(block, AXES, route)


def butterfly_sum(values):
    count = lax.axis_size(AXES)
    bit = 1
    while bit < count:
        route = [(i, i ^ bit) for i in range(count) if (i ^ bit) < count]
        values = values + lax.ppermute(values, AXES, route)
        bit *= 2
    return values


def row_major(array):
    return with_layout_constraint(array, Layout(major_to_minor=tuple(range(array.ndim))))


def small_lookup(table, index):
    return lax.dynamic_index_in_dim(table, index, 0, keepdims=False)


def table_entry(table, row, column):
    return small_lookup(small_lookup(table, row), column)


def per_device(state, left_env, right_env, site_ops, left_live, right_live):
    pairs = site_ops.shape[1]
    sec_size = state.shape[1]
    block_index = lax.axis_index("left") * lax.axis_size("right") + lax.axis_index("right")
    own_pair = block_index % pairs
    sector = block_index // pairs
    steps = (jnp.arange(pairs, dtype=jnp.int32) + 1) // 2
    own_step = small_lookup(steps, own_pair)
    positions = jnp.arange(sec_size, dtype=jnp.int32)
    row_mask = (positions < small_lookup(left_live, sector) * BLOCK).astype(jnp.float32)
    col_mask = (positions < small_lookup(right_live, sector + own_step) * BLOCK).astype(jnp.float32)
    live = row_mask[:, None] * col_mask[None, :]
    entries = float(state.shape[0] * sec_size * sec_size * lax.axis_size(AXES))

    masked = state[0] * live
    start_sum = butterfly_sum(jnp.sum(masked * masked))
    start_mean = start_sum / entries
    vector = masked / jnp.sqrt(start_mean + 1e-06)
    rounded = row_major(vector.astype(jnp.bfloat16))

    weights = []
    for offset in (2, 3):
        source_pair = (own_pair - offset) % pairs
        valid = block_index >= offset
        weights.append(
            jnp.where(
                valid, table_entry(site_ops[0], own_pair, source_pair), jnp.zeros((), jnp.float32)
            )
        )

    part_one = jnp.dot(rounded, right_env[1, 0], preferred_element_type=jnp.float32).astype(
        jnp.bfloat16
    )
    diag_weight = table_entry(site_ops[1], own_pair, own_pair)
    image_one = diag_weight * jnp.dot(left_env[1, 0], part_one, preferred_element_type=jnp.float32)

    rows = sec_size // CHUNKS
    pieces = [rounded[c * rows:(c + 1) * rows] for c in range(CHUNKS)]
    image_one, pieces[-1] = lax.optimization_barrier((image_one, pieces[-1]))
    parts = []
    for c in range(CHUNKS):
        far_two = shift_up(pieces[c], 2)
        far_three = shift_up(far_two, 1)
        source = (
            weights[0] * far_two.astype(jnp.float32) + weights[1] * far_three.astype(jnp.float32)
        ).astype(jnp.bfloat16)
        parts.append(
            jnp.dot(source, right_env[0, 0], preferred_element_type=jnp.float32).astype(jnp.bfloat16)
        )
    part_zero = jnp.concatenate(parts, axis=0)
    image = jnp.dot(left_env[0, 0], part_zero, preferred_element_type=jnp.float32) + image_one
    image = row_major(image * live)

    sums = butterfly_sum(jnp.stack([jnp.sum(vector * image), jnp.sum(image * image)]))
    alpha_value = sums[0] / entries
    vector_mean = start_mean / (start_mean + 1e-06)
    residual_mean = sums[1] / entries - alpha_value * alpha_value * (2.0 - vector_mean)
    residual = image - alpha_value * vector
    beta_value = jnp.sqrt(residual_mean + 1e-06)
    next_vector = residual / beta_value
    return (next_vector[None], jnp.stack([alpha_value, beta_value]))


def solution(mesh):
    in_specs = (
        P(AXES, None, None),
        P(None, AXES, None, None),
        P(None, AXES, None, None),
        P(),
        P(),
        P(),
    )
    out_specs = (P(AXES, None, None), P())
    return jax.shard_map(
        per_device, mesh=mesh, in_specs=in_specs, out_specs=out_specs, check_vma=False
    )
```

```python
import jax
import jax.numpy as jnp
from jax import lax
from jax.sharding import PartitionSpec as P
from jax.experimental.layout import Layout, with_layout_constraint

BLOCK = 256
AXES = ("left", "right")
CHUNKS = 4


def shift_up(block, distance):
    devices = range(lax.axis_size(AXES))
    route = [(i - distance, i) for i in devices if i - distance in devices]
    return lax.ppermute(block, AXES, route)


def butterfly_sum(values):
    count = lax.axis_size(AXES)
    bit = 1
    while bit < count:
        route = [(i, i ^ bit) for i in range(count) if (i ^ bit) < count]
        values = values + lax.ppermute(values, AXES, route)
        bit *= 2
    return values


def row_major(array):
    return with_layout_constraint(array, Layout(major_to_minor=tuple(range(array.ndim))))


def small_lookup(table, index):
    return lax.dynamic_index_in_dim(table, index, 0, keepdims=False)


def table_entry(table, row, column):
    return small_lookup(small_lookup(table, row), column)


def per_device(state, left_env, right_env, site_ops, left_live, right_live):
    pairs = site_ops.shape[1]
    sec_size = state.shape[1]
    block_index = lax.axis_index("left") * lax.axis_size("right") + lax.axis_index("right")
    own_pair = block_index % pairs
    sector = block_index // pairs
    steps = (jnp.arange(pairs, dtype=jnp.int32) + 1) // 2
    own_step = small_lookup(steps, own_pair)
    positions = jnp.arange(sec_size, dtype=jnp.int32)
    row_mask = (positions < small_lookup(left_live, sector) * BLOCK).astype(jnp.float32)
    col_mask = (positions < small_lookup(right_live, sector + own_step) * BLOCK).astype(jnp.float32)
    live = row_mask[:, None] * col_mask[None, :]
    entries = float(state.shape[0] * sec_size * sec_size * lax.axis_size(AXES))

    masked = state[0] * live
    column_sums = lax.optimization_barrier(jnp.sum(masked * masked, axis=0))
    start_sum = butterfly_sum(jnp.sum(column_sums))
    start_mean = start_sum / entries
    scale = jnp.sqrt(start_mean + 1e-06)
    vector = masked / scale
    rows = sec_size // CHUNKS
    pieces = [
        row_major((masked[c * rows:(c + 1) * rows] / scale).astype(jnp.bfloat16))
        for c in range(CHUNKS)
    ]
    rounded = jnp.concatenate(pieces, axis=0)

    weights = []
    for offset in (2, 3):
        source_pair = (own_pair - offset) % pairs
        valid = block_index >= offset
        weights.append(
            jnp.where(
                valid, table_entry(site_ops[0], own_pair, source_pair), jnp.zeros((), jnp.float32)
            )
        )

    part_one = jnp.dot(rounded, right_env[1, 0], preferred_element_type=jnp.float32).astype(
        jnp.bfloat16
    )
    diag_weight = table_entry(site_ops[1], own_pair, own_pair)
    image_one = diag_weight * jnp.dot(left_env[1, 0], part_one, preferred_element_type=jnp.float32)

    image_one, pieces[-1] = lax.optimization_barrier((image_one, pieces[-1]))
    parts = []
    for c in range(CHUNKS):
        far_two = shift_up(pieces[c], 2)
        far_three = shift_up(far_two, 1)
        source = (
            weights[0] * far_two.astype(jnp.float32) + weights[1] * far_three.astype(jnp.float32)
        ).astype(jnp.bfloat16)
        parts.append(
            jnp.dot(source, right_env[0, 0], preferred_element_type=jnp.float32).astype(jnp.bfloat16)
        )
    part_zero = jnp.concatenate(parts, axis=0)
    image = jnp.dot(left_env[0, 0], part_zero, preferred_element_type=jnp.float32) + image_one
    image = row_major(image * live)

    sums = butterfly_sum(jnp.stack([jnp.sum(vector * image), jnp.sum(image * image)]))
    alpha_value = sums[0] / entries
    vector_mean = start_mean / (start_mean + 1e-06)
    residual_mean = sums[1] / entries - alpha_value * alpha_value * (2.0 - vector_mean)
    residual = image - alpha_value * vector
    beta_value = jnp.sqrt(residual_mean + 1e-06)
    next_vector = residual / beta_value
    return (next_vector[None], jnp.stack([alpha_value, beta_value]))


def solution(mesh):
    in_specs = (
        P(AXES, None, None),
        P(None, AXES, None, None),
        P(None, AXES, None, None),
        P(),
        P(),
        P(),
    )
    out_specs = (P(AXES, None, None), P())
    return jax.shard_map(
        per_device, mesh=mesh, in_specs=in_specs, out_specs=out_specs, check_vma=False
    )
```

```python
import jax
import jax.numpy as jnp
from jax import lax
from jax.sharding import PartitionSpec as P
from jax.experimental.layout import Layout, with_layout_constraint

BLOCK = 256
AXES = ("left", "right")
CHUNKS = 4


def shift_up(block, distance):
    devices = range(lax.axis_size(AXES))
    route = [(i - distance, i) for i in devices if i - distance in devices]
    return lax.ppermute(block, AXES, route)


def all_sum(values):
    count = lax.axis_size(AXES)
    spread = jnp.broadcast_to(values[None], (count,) + values.shape)
    return jnp.sum(lax.all_to_all(spread, AXES, 0, 0, tiled=True), axis=0)


def row_major(array):
    return with_layout_constraint(array, Layout(major_to_minor=tuple(range(array.ndim))))


def small_lookup(table, index):
    return lax.dynamic_index_in_dim(table, index, 0, keepdims=False)


def table_entry(table, row, column):
    return small_lookup(small_lookup(table, row), column)


def per_device(state, left_env, right_env, site_ops, left_live, right_live):
    pairs = site_ops.shape[1]
    sec_size = state.shape[1]
    block_index = lax.axis_index("left") * lax.axis_size("right") + lax.axis_index("right")
    own_pair = block_index % pairs
    sector = block_index // pairs
    steps = (jnp.arange(pairs, dtype=jnp.int32) + 1) // 2
    own_step = small_lookup(steps, own_pair)
    positions = jnp.arange(sec_size, dtype=jnp.int32)
    row_mask = (positions < small_lookup(left_live, sector) * BLOCK).astype(jnp.float32)
    col_mask = (positions < small_lookup(right_live, sector + own_step) * BLOCK).astype(jnp.float32)
    live = row_mask[:, None] * col_mask[None, :]
    entries = float(state.shape[0] * sec_size * sec_size * lax.axis_size(AXES))

    masked = state[0] * live
    column_sums = lax.optimization_barrier(jnp.sum(masked * masked, axis=0))
    start_sum = all_sum(jnp.sum(column_sums)[None])[0]
    start_mean = start_sum / entries
    scale = jnp.sqrt(start_mean + 1e-06)
    vector = masked / scale
    rows = sec_size // CHUNKS
    pieces = [
        row_major((masked[c * rows:(c + 1) * rows] / scale).astype(jnp.bfloat16))
        for c in range(CHUNKS)
    ]
    rounded = jnp.concatenate(pieces, axis=0)

    weights = []
    for offset in (2, 3):
        source_pair = (own_pair - offset) % pairs
        valid = block_index >= offset
        weights.append(
            jnp.where(
                valid, table_entry(site_ops[0], own_pair, source_pair), jnp.zeros((), jnp.float32)
            )
        )

    part_one = jnp.dot(rounded, right_env[1, 0], preferred_element_type=jnp.float32).astype(
        jnp.bfloat16
    )
    diag_weight = table_entry(site_ops[1], own_pair, own_pair)
    image_one = diag_weight * jnp.dot(left_env[1, 0], part_one, preferred_element_type=jnp.float32)

    image_one, pieces[-1] = lax.optimization_barrier((image_one, pieces[-1]))
    parts = []
    for c in range(CHUNKS):
        far_two = shift_up(pieces[c], 2)
        far_three = shift_up(far_two, 1)
        source = (
            weights[0] * far_two.astype(jnp.float32) + weights[1] * far_three.astype(jnp.float32)
        ).astype(jnp.bfloat16)
        parts.append(
            jnp.dot(source, right_env[0, 0], preferred_element_type=jnp.float32).astype(jnp.bfloat16)
        )
    part_zero = jnp.concatenate(parts, axis=0)
    image = jnp.dot(left_env[0, 0], part_zero, preferred_element_type=jnp.float32) + image_one
    image = row_major(image * live)

    sums = all_sum(jnp.stack([jnp.sum(vector * image), jnp.sum(image * image)]))
    alpha_value = sums[0] / entries
    vector_mean = start_mean / (start_mean + 1e-06)
    residual_mean = sums[1] / entries - alpha_value * alpha_value * (2.0 - vector_mean)
    residual = image - alpha_value * vector
    beta_value = jnp.sqrt(residual_mean + 1e-06)
    next_vector = residual / beta_value
    return (next_vector[None], jnp.stack([alpha_value, beta_value]))


def solution(mesh):
    in_specs = (
        P(AXES, None, None),
        P(None, AXES, None, None),
        P(None, AXES, None, None),
        P(),
        P(),
        P(),
    )
    out_specs = (P(AXES, None, None), P())
    return jax.shard_map(
        per_device, mesh=mesh, in_specs=in_specs, out_specs=out_specs, check_vma=False
    )
```

```python
import jax
import jax.numpy as jnp
from jax import lax
from jax.sharding import PartitionSpec as P
from jax.experimental.layout import Layout, with_layout_constraint

BLOCK = 256
AXES = ("left", "right")
CHUNKS = 4


def shift_up(block, distance):
    devices = range(lax.axis_size(AXES))
    route = [(i - distance, i) for i in devices if i - distance in devices]
    return lax.ppermute(block, AXES, route)


def all_sum(values):
    count = lax.axis_size(AXES)
    spread = jnp.broadcast_to(values[None], (count,) + values.shape)
    return jnp.sum(lax.all_to_all(spread, AXES, 0, 0, tiled=True), axis=0)


def row_major(array):
    return with_layout_constraint(array, Layout(major_to_minor=tuple(range(array.ndim))))


def small_lookup(table, index):
    return lax.dynamic_index_in_dim(table, index, 0, keepdims=False)


def table_entry(table, row, column):
    return small_lookup(small_lookup(table, row), column)


def per_device(state, left_env, right_env, site_ops, left_live, right_live):
    pairs = site_ops.shape[1]
    sec_size = state.shape[1]
    block_index = lax.axis_index("left") * lax.axis_size("right") + lax.axis_index("right")
    own_pair = block_index % pairs
    sector = block_index // pairs
    steps = (jnp.arange(pairs, dtype=jnp.int32) + 1) // 2
    own_step = small_lookup(steps, own_pair)
    positions = jnp.arange(sec_size, dtype=jnp.int32)
    row_mask = (positions < small_lookup(left_live, sector) * BLOCK).astype(jnp.float32)
    col_mask = (positions < small_lookup(right_live, sector + own_step) * BLOCK).astype(jnp.float32)
    live = row_mask[:, None] * col_mask[None, :]
    entries = float(state.shape[0] * sec_size * sec_size * lax.axis_size(AXES))

    masked = state[0] * live
    column_sums = lax.optimization_barrier(jnp.sum(masked * masked, axis=0))
    start_sum = all_sum(jnp.sum(column_sums)[None])[0]
    start_mean = start_sum / entries
    scale = jnp.sqrt(start_mean + 1e-06)
    vector = masked / scale
    rows = sec_size // CHUNKS
    pieces = [
        row_major((masked[c * rows:(c + 1) * rows] / scale).astype(jnp.bfloat16))
        for c in range(CHUNKS)
    ]
    rounded = jnp.concatenate(pieces, axis=0)

    weights = []
    for offset in (2, 3):
        source_pair = (own_pair - offset) % pairs
        valid = block_index >= offset
        weights.append(
            jnp.where(
                valid, table_entry(site_ops[0], own_pair, source_pair), jnp.zeros((), jnp.float32)
            )
        )

    part_one = jnp.dot(rounded, right_env[1, 0], preferred_element_type=jnp.float32).astype(
        jnp.bfloat16
    )
    diag_weight = table_entry(site_ops[1], own_pair, own_pair)
    image_one = diag_weight * jnp.dot(left_env[1, 0], part_one, preferred_element_type=jnp.float32)

    image_one, pieces[-1] = lax.optimization_barrier((image_one, pieces[-1]))
    parts = []
    for c in range(CHUNKS):
        far_two = shift_up(pieces[c], 2)
        far_three = shift_up(far_two, 1)
        source = (
            weights[0] * far_two.astype(jnp.float32) + weights[1] * far_three.astype(jnp.float32)
        ).astype(jnp.bfloat16)
        parts.append(
            jnp.dot(source, right_env[0, 0], preferred_element_type=jnp.float32).astype(jnp.bfloat16)
        )
    early = (CHUNKS - 1) * rows
    image = image_one + jnp.dot(
        left_env[0, 0][:, :early], jnp.concatenate(parts[:-1], axis=0),
        preferred_element_type=jnp.float32,
    )
    image = image + jnp.dot(
        left_env[0, 0][:, early:], parts[-1], preferred_element_type=jnp.float32
    )
    image = row_major(image * live)

    sums = all_sum(jnp.stack([jnp.sum(vector * image), jnp.sum(image * image)]))
    alpha_value = sums[0] / entries
    vector_mean = start_mean / (start_mean + 1e-06)
    residual_mean = sums[1] / entries - alpha_value * alpha_value * (2.0 - vector_mean)
    residual = image - alpha_value * vector
    beta_value = jnp.sqrt(residual_mean + 1e-06)
    next_vector = residual / beta_value
    return (next_vector[None], jnp.stack([alpha_value, beta_value]))


def solution(mesh):
    in_specs = (
        P(AXES, None, None),
        P(None, AXES, None, None),
        P(None, AXES, None, None),
        P(),
        P(),
        P(),
    )
    out_specs = (P(AXES, None, None), P())
    return jax.shard_map(
        per_device, mesh=mesh, in_specs=in_specs, out_specs=out_specs, check_vma=False
    )
```

```python
import functools

import jax
import jax.numpy as jnp
from jax import lax
from jax.sharding import PartitionSpec as P
from jax.experimental.layout import Layout, with_layout_constraint
from jax.experimental import pallas as pl
from jax.experimental.pallas import tpu as pltpu

BLOCK = 256
AXES = ("left", "right")
CHUNKS = 4


def shift_up(block, distance):
    devices = range(lax.axis_size(AXES))
    route = [(i - distance, i) for i in devices if i - distance in devices]
    return lax.ppermute(block, AXES, route)


def all_sum(values):
    count = lax.axis_size(AXES)
    spread = jnp.broadcast_to(values[None], (count,) + values.shape)
    return jnp.sum(lax.all_to_all(spread, AXES, 0, 0, tiled=True), axis=0)


def square_sum_kernel(pairs, index_ref, left_ref, right_ref, state_ref, out_ref, acc_ref):
    step = pl.program_id(0)
    rows, cols = state_ref.shape[1], state_ref.shape[2]
    sector = index_ref[0] // pairs
    pair = index_ref[0] % pairs
    row_limit = left_ref[sector] * BLOCK
    col_limit = right_ref[sector + (pair + 1) // 2] * BLOCK

    @pl.when(step == 0)
    def _():
        acc_ref[...] = jnp.zeros_like(acc_ref)

    x = state_ref[0]
    row_ids = step * rows + lax.broadcasted_iota(jnp.int32, (rows, cols), 0)
    col_ids = lax.broadcasted_iota(jnp.int32, (rows, cols), 1)
    x = jnp.where((row_ids < row_limit) & (col_ids < col_limit), x, 0.0)
    acc_ref[...] += jnp.sum((x * x).reshape(rows // 8, 8, cols), axis=0)

    @pl.when(step == pl.num_programs(0) - 1)
    def _():
        out_ref[0, 0] = jnp.sum(acc_ref[...])


def masked_square_sum(pairs, block_index, left_live, right_live, state):
    sec_size = state.shape[1]
    rows = 256
    return pl.pallas_call(
        functools.partial(square_sum_kernel, pairs),
        grid_spec=pltpu.PrefetchScalarGridSpec(
            num_scalar_prefetch=3,
            grid=(sec_size // rows,),
            in_specs=[pl.BlockSpec((1, rows, sec_size), lambda i, *_: (0, i, 0))],
            out_specs=pl.BlockSpec(memory_space=pltpu.SMEM),
            scratch_shapes=[pltpu.VMEM((8, sec_size), jnp.float32)],
        ),
        out_shape=jax.ShapeDtypeStruct((1, 1), jnp.float32),
    )(block_index.reshape(1), left_live, right_live, state)


def row_major(array):
    return with_layout_constraint(array, Layout(major_to_minor=tuple(range(array.ndim))))


def small_lookup(table, index):
    return lax.dynamic_index_in_dim(table, index, 0, keepdims=False)


def table_entry(table, row, column):
    return small_lookup(small_lookup(table, row), column)


def per_device(state, left_env, right_env, site_ops, left_live, right_live):
    pairs = site_ops.shape[1]
    sec_size = state.shape[1]
    block_index = lax.axis_index("left") * lax.axis_size("right") + lax.axis_index("right")
    own_pair = block_index % pairs
    sector = block_index // pairs
    steps = (jnp.arange(pairs, dtype=jnp.int32) + 1) // 2
    own_step = small_lookup(steps, own_pair)
    positions = jnp.arange(sec_size, dtype=jnp.int32)
    row_mask = (positions < small_lookup(left_live, sector) * BLOCK).astype(jnp.float32)
    col_mask = (positions < small_lookup(right_live, sector + own_step) * BLOCK).astype(jnp.float32)
    live = row_mask[:, None] * col_mask[None, :]
    entries = float(state.shape[0] * sec_size * sec_size * lax.axis_size(AXES))

    masked = state[0] * live
    start_sum = all_sum(
        masked_square_sum(pairs, block_index.astype(jnp.int32), left_live, right_live, state)[0]
    )[0]
    start_mean = start_sum / entries
    scale = jnp.sqrt(start_mean + 1e-06)
    vector = masked / scale
    rows = sec_size // CHUNKS
    pieces = [
        row_major((masked[c * rows:(c + 1) * rows] / scale).astype(jnp.bfloat16))
        for c in range(CHUNKS)
    ]
    rounded = jnp.concatenate(pieces, axis=0)

    weights = []
    for offset in (2, 3):
        source_pair = (own_pair - offset) % pairs
        valid = block_index >= offset
        weights.append(
            jnp.where(
                valid, table_entry(site_ops[0], own_pair, source_pair), jnp.zeros((), jnp.float32)
            )
        )

    part_one = jnp.dot(rounded, right_env[1, 0], preferred_element_type=jnp.float32).astype(
        jnp.bfloat16
    )
    diag_weight = table_entry(site_ops[1], own_pair, own_pair)
    image_one = diag_weight * jnp.dot(left_env[1, 0], part_one, preferred_element_type=jnp.float32)

    image_one, pieces[-1] = lax.optimization_barrier((image_one, pieces[-1]))
    parts = []
    for c in range(CHUNKS):
        far_two = shift_up(pieces[c], 2)
        far_three = shift_up(far_two, 1)
        source = (
            weights[0] * far_two.astype(jnp.float32) + weights[1] * far_three.astype(jnp.float32)
        ).astype(jnp.bfloat16)
        parts.append(
            jnp.dot(source, right_env[0, 0], preferred_element_type=jnp.float32).astype(jnp.bfloat16)
        )
    part_zero = jnp.concatenate(parts, axis=0)
    image = jnp.dot(left_env[0, 0], part_zero, preferred_element_type=jnp.float32) + image_one
    image = row_major(image * live)

    sums = all_sum(jnp.stack([jnp.sum(vector * image), jnp.sum(image * image)]))
    alpha_value = sums[0] / entries
    vector_mean = start_mean / (start_mean + 1e-06)
    residual_mean = sums[1] / entries - alpha_value * alpha_value * (2.0 - vector_mean)
    residual = image - alpha_value * vector
    beta_value = jnp.sqrt(residual_mean + 1e-06)
    next_vector = residual / beta_value
    return (next_vector[None], jnp.stack([alpha_value, beta_value]))


def solution(mesh):
    in_specs = (
        P(AXES, None, None),
        P(None, AXES, None, None),
        P(None, AXES, None, None),
        P(),
        P(),
        P(),
    )
    out_specs = (P(AXES, None, None), P())
    return jax.shard_map(
        per_device, mesh=mesh, in_specs=in_specs, out_specs=out_specs, check_vma=False
    )
```

```python
import functools

import jax
import jax.numpy as jnp
from jax import lax
from jax.sharding import PartitionSpec as P
from jax.experimental.layout import Layout, with_layout_constraint
from jax.experimental import pallas as pl
from jax.experimental.pallas import tpu as pltpu

BLOCK = 256
AXES = ("left", "right")
CHUNKS = 4


def shift_up(block, distance):
    devices = range(lax.axis_size(AXES))
    route = [(i - distance, i) for i in devices if i - distance in devices]
    return lax.ppermute(block, AXES, route)


def all_sum(values):
    count = lax.axis_size(AXES)
    return exchange_sum(jnp.broadcast_to(values[None], (count,) + values.shape))


def exchange_sum(spread):
    return jnp.sum(lax.all_to_all(spread, AXES, 0, 0, tiled=True), axis=0)


def square_sum_kernel(pairs, index_ref, left_ref, right_ref, state_ref, out_ref, acc_ref):
    step = pl.program_id(0)
    rows, cols = state_ref.shape[1], state_ref.shape[2]
    sector = index_ref[0] // pairs
    pair = index_ref[0] % pairs
    row_limit = left_ref[sector] * BLOCK
    col_limit = right_ref[sector + (pair + 1) // 2] * BLOCK

    @pl.when(step == 0)
    def _():
        acc_ref[...] = jnp.zeros_like(acc_ref)

    x = state_ref[0]
    row_ids = step * rows + lax.broadcasted_iota(jnp.int32, (rows, cols), 0)
    col_ids = lax.broadcasted_iota(jnp.int32, (rows, cols), 1)
    x = jnp.where((row_ids < row_limit) & (col_ids < col_limit), x, 0.0)
    acc_ref[...] += jnp.sum((x * x).reshape(rows // 8, 8, cols), axis=0)

    @pl.when(step == pl.num_programs(0) - 1)
    def _():
        out_ref[...] = jnp.full(out_ref.shape, jnp.sum(acc_ref[...]), jnp.float32)


def masked_square_sum(pairs, block_index, left_live, right_live, state):
    count = lax.axis_size(AXES)
    sec_size = state.shape[1]
    rows = 256
    return pl.pallas_call(
        functools.partial(square_sum_kernel, pairs),
        grid_spec=pltpu.PrefetchScalarGridSpec(
            num_scalar_prefetch=3,
            grid=(sec_size // rows,),
            in_specs=[pl.BlockSpec((1, rows, sec_size), lambda i, *_: (0, i, 0))],
            out_specs=pl.BlockSpec((count, 1, 1), lambda i, *_: (0, 0, 0)),
            scratch_shapes=[pltpu.VMEM((8, sec_size), jnp.float32)],
        ),
        out_shape=jax.ShapeDtypeStruct((count, 1, 1), jnp.float32),
    )(block_index.reshape(1), left_live, right_live, state)


def row_major(array):
    return with_layout_constraint(array, Layout(major_to_minor=tuple(range(array.ndim))))


def small_lookup(table, index):
    return lax.dynamic_index_in_dim(table, index, 0, keepdims=False)


def table_entry(table, row, column):
    return small_lookup(small_lookup(table, row), column)


def per_device(state, left_env, right_env, site_ops, left_live, right_live):
    pairs = site_ops.shape[1]
    sec_size = state.shape[1]
    block_index = lax.axis_index("left") * lax.axis_size("right") + lax.axis_index("right")
    own_pair = block_index % pairs
    sector = block_index // pairs
    steps = (jnp.arange(pairs, dtype=jnp.int32) + 1) // 2
    own_step = small_lookup(steps, own_pair)
    positions = jnp.arange(sec_size, dtype=jnp.int32)
    row_mask = (positions < small_lookup(left_live, sector) * BLOCK).astype(jnp.float32)
    col_mask = (positions < small_lookup(right_live, sector + own_step) * BLOCK).astype(jnp.float32)
    live = row_mask[:, None] * col_mask[None, :]
    entries = float(state.shape[0] * sec_size * sec_size * lax.axis_size(AXES))

    masked = state[0] * live
    start_sum = exchange_sum(
        masked_square_sum(pairs, block_index.astype(jnp.int32), left_live, right_live, state)
    )[0, 0]
    start_mean = start_sum / entries
    scale = jnp.sqrt(start_mean + 1e-06)
    vector = masked / scale
    rows = sec_size // CHUNKS
    pieces = [
        row_major((masked[c * rows:(c + 1) * rows] / scale).astype(jnp.bfloat16))
        for c in range(CHUNKS)
    ]
    rounded = jnp.concatenate(pieces, axis=0)

    weights = []
    for offset in (2, 3):
        source_pair = (own_pair - offset) % pairs
        valid = block_index >= offset
        weights.append(
            jnp.where(
                valid, table_entry(site_ops[0], own_pair, source_pair), jnp.zeros((), jnp.float32)
            )
        )

    part_one = jnp.dot(rounded, right_env[1, 0], preferred_element_type=jnp.float32).astype(
        jnp.bfloat16
    )
    diag_weight = table_entry(site_ops[1], own_pair, own_pair)
    image_one = diag_weight * jnp.dot(left_env[1, 0], part_one, preferred_element_type=jnp.float32)

    image_one, pieces[-1] = lax.optimization_barrier((image_one, pieces[-1]))
    parts = []
    for c in range(CHUNKS):
        far_two = shift_up(pieces[c], 2)
        far_three = shift_up(far_two, 1)
        source = (
            weights[0] * far_two.astype(jnp.float32) + weights[1] * far_three.astype(jnp.float32)
        ).astype(jnp.bfloat16)
        parts.append(
            jnp.dot(source, right_env[0, 0], preferred_element_type=jnp.float32).astype(jnp.bfloat16)
        )
    part_zero = jnp.concatenate(parts, axis=0)
    image = jnp.dot(left_env[0, 0], part_zero, preferred_element_type=jnp.float32) + image_one
    image = row_major(image * live)

    sums = all_sum(jnp.stack([jnp.sum(vector * image), jnp.sum(image * image)]))
    alpha_value = sums[0] / entries
    vector_mean = start_mean / (start_mean + 1e-06)
    residual_mean = sums[1] / entries - alpha_value * alpha_value * (2.0 - vector_mean)
    residual = image - alpha_value * vector
    beta_value = jnp.sqrt(residual_mean + 1e-06)
    next_vector = residual / beta_value
    return (next_vector[None], jnp.stack([alpha_value, beta_value]))


def solution(mesh):
    in_specs = (
        P(AXES, None, None),
        P(None, AXES, None, None),
        P(None, AXES, None, None),
        P(),
        P(),
        P(),
    )
    out_specs = (P(AXES, None, None), P())
    return jax.shard_map(
        per_device, mesh=mesh, in_specs=in_specs, out_specs=out_specs, check_vma=False
    )
```

```python
import functools

import jax
import jax.numpy as jnp
from jax import lax
from jax.sharding import PartitionSpec as P
from jax.experimental.layout import Layout, with_layout_constraint
from jax.experimental import pallas as pl
from jax.experimental.pallas import tpu as pltpu

BLOCK = 256
AXES = ("left", "right")
CHUNKS = 4


def shift_up(block, distance):
    devices = range(lax.axis_size(AXES))
    route = [(i - distance, i) for i in devices if i - distance in devices]
    return lax.ppermute(block, AXES, route)


def all_sum(values):
    count = lax.axis_size(AXES)
    return exchange_sum(jnp.broadcast_to(values[None], (count,) + values.shape))


def exchange_sum(spread):
    return jnp.sum(lax.all_to_all(spread, AXES, 0, 0, tiled=True), axis=0)


def square_sum_kernel(pairs, index_ref, left_ref, right_ref, state_ref, out_ref, acc_ref):
    step = pl.program_id(0)
    rows, cols = state_ref.shape[1], state_ref.shape[2]
    sector = index_ref[0] // pairs
    pair = index_ref[0] % pairs
    row_limit = left_ref[sector] * BLOCK
    col_limit = right_ref[sector + (pair + 1) // 2] * BLOCK

    @pl.when(step == 0)
    def _():
        acc_ref[...] = jnp.zeros_like(acc_ref)

    x = state_ref[0]
    row_ids = step * rows + lax.broadcasted_iota(jnp.int32, (rows, cols), 0)
    col_ids = lax.broadcasted_iota(jnp.int32, (rows, cols), 1)
    x = jnp.where((row_ids < row_limit) & (col_ids < col_limit), x, 0.0)
    acc_ref[...] += jnp.sum((x * x).reshape(rows // 8, 8, cols), axis=0)

    @pl.when(step == pl.num_programs(0) - 1)
    def _():
        out_ref[...] = jnp.full(out_ref.shape, jnp.sum(acc_ref[...]), jnp.float32)


def masked_square_sum(pairs, block_index, left_live, right_live, state):
    count = lax.axis_size(AXES)
    sec_size = state.shape[1]
    rows = 256
    return pl.pallas_call(
        functools.partial(square_sum_kernel, pairs),
        grid_spec=pltpu.PrefetchScalarGridSpec(
            num_scalar_prefetch=3,
            grid=(sec_size // rows,),
            in_specs=[pl.BlockSpec((1, rows, sec_size), lambda i, *_: (0, i, 0))],
            out_specs=pl.BlockSpec((count, 1, 1), lambda i, *_: (0, 0, 0)),
            scratch_shapes=[pltpu.VMEM((8, sec_size), jnp.float32)],
        ),
        out_shape=jax.ShapeDtypeStruct((count, 1, 1), jnp.float32),
    )(block_index.reshape(1), left_live, right_live, state)


def live_limits(pairs, index_ref, left_ref, right_ref):
    sector = index_ref[0] // pairs
    pair = index_ref[0] % pairs
    return left_ref[sector] * BLOCK, right_ref[sector + (pair + 1) // 2] * BLOCK


def image_kernel(pairs, index_ref, left_ref, right_ref, scale_ref, env_ref, part_ref, one_ref,
                 state_ref, image_ref, sums_ref, acc_ref):
    step = pl.program_id(0)
    rows, cols = one_ref.shape
    row_limit, col_limit = live_limits(pairs, index_ref, left_ref, right_ref)

    @pl.when(step == 0)
    def _():
        acc_ref[...] = jnp.zeros_like(acc_ref)

    row_ids = step * rows + lax.broadcasted_iota(jnp.int32, (rows, cols), 0)
    col_ids = lax.broadcasted_iota(jnp.int32, (rows, cols), 1)
    live = ((row_ids < row_limit) & (col_ids < col_limit)).astype(jnp.float32)
    image = jnp.dot(env_ref[...], part_ref[...], preferred_element_type=jnp.float32) + one_ref[...]
    image = image * live
    image_ref[...] = image
    vector = state_ref[0] * live / scale_ref[0]
    acc_ref[0] += jnp.sum((vector * image).reshape(rows // 8, 8, cols), axis=0)
    acc_ref[1] += jnp.sum((image * image).reshape(rows // 8, 8, cols), axis=0)

    @pl.when(step == pl.num_programs(0) - 1)
    def _():
        which = lax.broadcasted_iota(jnp.int32, sums_ref.shape, 2)
        sums_ref[...] = jnp.where(which == 0, jnp.sum(acc_ref[0]), jnp.sum(acc_ref[1]))


def masked_image(pairs, block_index, left_live, right_live, scale, left_zero, part_zero,
                 image_one, state):
    count = lax.axis_size(AXES)
    sec_size = state.shape[1]
    rows = 256
    return pl.pallas_call(
        functools.partial(image_kernel, pairs),
        grid_spec=pltpu.PrefetchScalarGridSpec(
            num_scalar_prefetch=3,
            grid=(sec_size // rows,),
            in_specs=[
                pl.BlockSpec(memory_space=pltpu.SMEM),
                pl.BlockSpec((rows, sec_size), lambda i, *_: (i, 0)),
                pl.BlockSpec((sec_size, sec_size), lambda i, *_: (0, 0)),
                pl.BlockSpec((rows, sec_size), lambda i, *_: (i, 0)),
                pl.BlockSpec((1, rows, sec_size), lambda i, *_: (0, i, 0)),
            ],
            out_specs=[
                pl.BlockSpec((rows, sec_size), lambda i, *_: (i, 0)),
                pl.BlockSpec((count, 1, 2), lambda i, *_: (0, 0, 0)),
            ],
            scratch_shapes=[pltpu.VMEM((2, 8, sec_size), jnp.float32)],
        ),
        out_shape=[
            jax.ShapeDtypeStruct((sec_size, sec_size), jnp.float32),
            jax.ShapeDtypeStruct((count, 1, 2), jnp.float32),
        ],
    )(block_index.reshape(1), left_live, right_live, scale.reshape(1), left_zero, part_zero,
      image_one, state)


def row_major(array):
    return with_layout_constraint(array, Layout(major_to_minor=tuple(range(array.ndim))))


def small_lookup(table, index):
    return lax.dynamic_index_in_dim(table, index, 0, keepdims=False)


def table_entry(table, row, column):
    return small_lookup(small_lookup(table, row), column)


def per_device(state, left_env, right_env, site_ops, left_live, right_live):
    pairs = site_ops.shape[1]
    sec_size = state.shape[1]
    block_index = lax.axis_index("left") * lax.axis_size("right") + lax.axis_index("right")
    own_pair = block_index % pairs
    sector = block_index // pairs
    steps = (jnp.arange(pairs, dtype=jnp.int32) + 1) // 2
    own_step = small_lookup(steps, own_pair)
    positions = jnp.arange(sec_size, dtype=jnp.int32)
    row_mask = (positions < small_lookup(left_live, sector) * BLOCK).astype(jnp.float32)
    col_mask = (positions < small_lookup(right_live, sector + own_step) * BLOCK).astype(jnp.float32)
    live = row_mask[:, None] * col_mask[None, :]
    entries = float(state.shape[0] * sec_size * sec_size * lax.axis_size(AXES))

    masked = state[0] * live
    start_sum = exchange_sum(
        masked_square_sum(pairs, block_index.astype(jnp.int32), left_live, right_live, state)
    )[0, 0]
    start_mean = start_sum / entries
    scale = jnp.sqrt(start_mean + 1e-06)
    vector = masked / scale
    rows = sec_size // CHUNKS
    pieces = [
        row_major((masked[c * rows:(c + 1) * rows] / scale).astype(jnp.bfloat16))
        for c in range(CHUNKS)
    ]
    rounded = jnp.concatenate(pieces, axis=0)

    weights = []
    for offset in (2, 3):
        source_pair = (own_pair - offset) % pairs
        valid = block_index >= offset
        weights.append(
            jnp.where(
                valid, table_entry(site_ops[0], own_pair, source_pair), jnp.zeros((), jnp.float32)
            )
        )

    part_one = jnp.dot(rounded, right_env[1, 0], preferred_element_type=jnp.float32).astype(
        jnp.bfloat16
    )
    diag_weight = table_entry(site_ops[1], own_pair, own_pair)
    image_one = diag_weight * jnp.dot(left_env[1, 0], part_one, preferred_element_type=jnp.float32)

    image_one, pieces[-1] = lax.optimization_barrier((image_one, pieces[-1]))
    parts = []
    for c in range(CHUNKS):
        far_two = shift_up(pieces[c], 2)
        far_three = shift_up(far_two, 1)
        source = (
            weights[0] * far_two.astype(jnp.float32) + weights[1] * far_three.astype(jnp.float32)
        ).astype(jnp.bfloat16)
        parts.append(
            jnp.dot(source, right_env[0, 0], preferred_element_type=jnp.float32).astype(jnp.bfloat16)
        )
    part_zero = jnp.concatenate(parts, axis=0)
    image, spread = masked_image(
        pairs, block_index.astype(jnp.int32), left_live, right_live, scale, left_env[0, 0],
        part_zero, image_one, state,
    )
    sums = exchange_sum(spread)[0]
    alpha_value = sums[0] / entries
    vector_mean = start_mean / (start_mean + 1e-06)
    residual_mean = sums[1] / entries - alpha_value * alpha_value * (2.0 - vector_mean)
    residual = image - alpha_value * vector
    beta_value = jnp.sqrt(residual_mean + 1e-06)
    next_vector = residual / beta_value
    return (next_vector[None], jnp.stack([alpha_value, beta_value]))


def solution(mesh):
    in_specs = (
        P(AXES, None, None),
        P(None, AXES, None, None),
        P(None, AXES, None, None),
        P(),
        P(),
        P(),
    )
    out_specs = (P(AXES, None, None), P())
    return jax.shard_map(
        per_device, mesh=mesh, in_specs=in_specs, out_specs=out_specs, check_vma=False
    )
```

```python
import functools

import jax
import jax.numpy as jnp
from jax import lax
from jax.sharding import PartitionSpec as P
from jax.experimental.layout import Layout, with_layout_constraint
from jax.experimental import pallas as pl
from jax.experimental.pallas import tpu as pltpu

BLOCK = 256
AXES = ("left", "right")
CHUNKS = 4


def shift_up(block, distance):
    devices = range(lax.axis_size(AXES))
    route = [(i - distance, i) for i in devices if i - distance in devices]
    return lax.ppermute(block, AXES, route)


def all_sum(values):
    count = lax.axis_size(AXES)
    return exchange_sum(jnp.broadcast_to(values[None], (count,) + values.shape))


def exchange_sum(spread):
    return jnp.sum(lax.all_to_all(spread, AXES, 0, 0, tiled=True), axis=0)


def square_sum_kernel(pairs, index_ref, left_ref, right_ref, state_ref, out_ref, acc_ref):
    step = pl.program_id(0)
    rows, cols = state_ref.shape[1], state_ref.shape[2]
    sector = index_ref[0] // pairs
    pair = index_ref[0] % pairs
    row_limit = left_ref[sector] * BLOCK
    col_limit = right_ref[sector + (pair + 1) // 2] * BLOCK

    @pl.when(step == 0)
    def _():
        acc_ref[...] = jnp.zeros_like(acc_ref)

    x = state_ref[0]
    row_ids = step * rows + lax.broadcasted_iota(jnp.int32, (rows, cols), 0)
    col_ids = lax.broadcasted_iota(jnp.int32, (rows, cols), 1)
    x = jnp.where((row_ids < row_limit) & (col_ids < col_limit), x, 0.0)
    acc_ref[...] += jnp.sum((x * x).reshape(rows // 8, 8, cols), axis=0)

    @pl.when(step == pl.num_programs(0) - 1)
    def _():
        out_ref[...] = jnp.full(out_ref.shape, jnp.sum(acc_ref[...]), jnp.float32)


def masked_square_sum(pairs, block_index, left_live, right_live, state):
    count = lax.axis_size(AXES)
    sec_size = state.shape[1]
    rows = 256
    return pl.pallas_call(
        functools.partial(square_sum_kernel, pairs),
        grid_spec=pltpu.PrefetchScalarGridSpec(
            num_scalar_prefetch=3,
            grid=(sec_size // rows,),
            in_specs=[pl.BlockSpec((1, rows, sec_size), lambda i, *_: (0, i, 0))],
            out_specs=pl.BlockSpec((count, 1, 1), lambda i, *_: (0, 0, 0)),
            scratch_shapes=[pltpu.VMEM((8, sec_size), jnp.float32)],
        ),
        out_shape=jax.ShapeDtypeStruct((count, 1, 1), jnp.float32),
    )(block_index.reshape(1), left_live, right_live, state)


def row_major(array):
    return with_layout_constraint(array, Layout(major_to_minor=tuple(range(array.ndim))))


def small_lookup(table, index):
    return lax.dynamic_index_in_dim(table, index, 0, keepdims=False)


def table_entry(table, row, column):
    return small_lookup(small_lookup(table, row), column)


def per_device(state, left_env, right_env, site_ops, left_live, right_live):
    pairs = site_ops.shape[1]
    sec_size = state.shape[1]
    block_index = lax.axis_index("left") * lax.axis_size("right") + lax.axis_index("right")
    own_pair = block_index % pairs
    sector = block_index // pairs
    steps = (jnp.arange(pairs, dtype=jnp.int32) + 1) // 2
    own_step = small_lookup(steps, own_pair)
    positions = jnp.arange(sec_size, dtype=jnp.int32)
    row_mask = (positions < small_lookup(left_live, sector) * BLOCK).astype(jnp.float32)
    col_mask = (positions < small_lookup(right_live, sector + own_step) * BLOCK).astype(jnp.float32)
    live = row_mask[:, None] * col_mask[None, :]
    entries = float(state.shape[0] * sec_size * sec_size * lax.axis_size(AXES))

    masked = state[0] * live
    start_sum = exchange_sum(
        masked_square_sum(pairs, block_index.astype(jnp.int32), left_live, right_live, state)
    )[0, 0]
    start_mean = start_sum / entries
    scale = jnp.sqrt(start_mean + 1e-06)
    vector = masked / scale
    rows = sec_size // CHUNKS
    pieces = [
        row_major((masked[c * rows:(c + 1) * rows] / scale).astype(jnp.bfloat16))
        for c in range(CHUNKS)
    ]
    rounded = jnp.concatenate(pieces, axis=0)

    weights = []
    for offset in (2, 3):
        source_pair = (own_pair - offset) % pairs
        valid = block_index >= offset
        weights.append(
            jnp.where(
                valid, table_entry(site_ops[0], own_pair, source_pair), jnp.zeros((), jnp.float32)
            )
        )

    part_one = jnp.dot(rounded, right_env[1, 0], preferred_element_type=jnp.float32).astype(
        jnp.bfloat16
    )
    diag_weight = table_entry(site_ops[1], own_pair, own_pair)
    image_one = diag_weight * jnp.dot(left_env[1, 0], part_one, preferred_element_type=jnp.float32)

    image_one, pieces[-1] = lax.optimization_barrier((image_one, pieces[-1]))
    parts = []
    for c in range(CHUNKS):
        far_two = shift_up(pieces[c], 2)
        far_three = shift_up(far_two, 1)
        source = (
            weights[0] * far_two.astype(jnp.float32) + weights[1] * far_three.astype(jnp.float32)
        ).astype(jnp.bfloat16)
        parts.append(
            jnp.dot(source, right_env[0, 0], preferred_element_type=jnp.float32).astype(jnp.bfloat16)
        )
    part_zero = jnp.concatenate(parts, axis=0)
    image = jnp.dot(left_env[0, 0], part_zero, preferred_element_type=jnp.float32) + image_one
    image = row_major(image * live)

    sums = all_sum(jnp.sum(jnp.stack([vector * image, image * image]), axis=(1, 2)))
    alpha_value = sums[0:1] / entries
    vector_mean = start_mean / (start_mean + 1e-06)
    residual_mean = sums[1:2] / entries - alpha_value * alpha_value * (2.0 - vector_mean)
    beta_value = jnp.sqrt(residual_mean + 1e-06)
    residual = image - alpha_value[:, None] * vector
    next_vector = residual / beta_value[:, None]
    return (next_vector[None], jnp.concatenate([alpha_value, beta_value]))


def solution(mesh):
    in_specs = (
        P(AXES, None, None),
        P(None, AXES, None, None),
        P(None, AXES, None, None),
        P(),
        P(),
        P(),
    )
    out_specs = (P(AXES, None, None), P())
    return jax.shard_map(
        per_device, mesh=mesh, in_specs=in_specs, out_specs=out_specs, check_vma=False
    )
```

```python
import functools

import jax
import jax.numpy as jnp
from jax import lax
from jax.sharding import PartitionSpec as P
from jax.experimental.layout import Layout, with_layout_constraint
from jax.experimental import pallas as pl
from jax.experimental.pallas import tpu as pltpu

BLOCK = 256
AXES = ("left", "right")
CHUNKS = 4


def shift_up(block, distance):
    devices = range(lax.axis_size(AXES))
    route = [(i - distance, i) for i in devices if i - distance in devices]
    return lax.ppermute(block, AXES, route)


def all_sum(values):
    count = lax.axis_size(AXES)
    return exchange_sum(jnp.broadcast_to(values[None], (count,) + values.shape))


def exchange_sum(spread):
    return jnp.sum(lax.all_to_all(spread, AXES, 0, 0, tiled=True), axis=0)


def square_sum_kernel(pairs, index_ref, left_ref, right_ref, state_ref, out_ref, acc_ref):
    step = pl.program_id(0)
    rows, cols = state_ref.shape[1], state_ref.shape[2]
    sector = index_ref[0] // pairs
    pair = index_ref[0] % pairs
    row_limit = left_ref[sector] * BLOCK
    col_limit = right_ref[sector + (pair + 1) // 2] * BLOCK

    @pl.when(step == 0)
    def _():
        acc_ref[...] = jnp.zeros_like(acc_ref)

    x = state_ref[0]
    row_ids = step * rows + lax.broadcasted_iota(jnp.int32, (rows, cols), 0)
    col_ids = lax.broadcasted_iota(jnp.int32, (rows, cols), 1)
    x = jnp.where((row_ids < row_limit) & (col_ids < col_limit), x, 0.0)
    acc_ref[...] += jnp.sum((x * x).reshape(rows // 8, 8, cols), axis=0)

    @pl.when(step == pl.num_programs(0) - 1)
    def _():
        out_ref[...] = jnp.full(out_ref.shape, jnp.sum(acc_ref[...]), jnp.float32)


def masked_square_sum(pairs, block_index, left_live, right_live, state):
    count = lax.axis_size(AXES)
    sec_size = state.shape[1]
    rows = 256
    return pl.pallas_call(
        functools.partial(square_sum_kernel, pairs),
        grid_spec=pltpu.PrefetchScalarGridSpec(
            num_scalar_prefetch=3,
            grid=(sec_size // rows,),
            in_specs=[pl.BlockSpec((1, rows, sec_size), lambda i, *_: (0, i, 0))],
            out_specs=pl.BlockSpec((count, 1, 1), lambda i, *_: (0, 0, 0)),
            scratch_shapes=[pltpu.VMEM((8, sec_size), jnp.float32)],
        ),
        out_shape=jax.ShapeDtypeStruct((count, 1, 1), jnp.float32),
    )(block_index.reshape(1), left_live, right_live, state)


def row_major(array):
    return with_layout_constraint(array, Layout(major_to_minor=tuple(range(array.ndim))))


def small_lookup(table, index):
    return lax.dynamic_index_in_dim(table, index, 0, keepdims=False)


def table_entry(table, row, column):
    return small_lookup(small_lookup(table, row), column)


def per_device(state, left_env, right_env, site_ops, left_live, right_live):
    pairs = site_ops.shape[1]
    sec_size = state.shape[1]
    block_index = lax.axis_index("left") * lax.axis_size("right") + lax.axis_index("right")
    own_pair = block_index % pairs
    sector = block_index // pairs
    steps = (jnp.arange(pairs, dtype=jnp.int32) + 1) // 2
    own_step = small_lookup(steps, own_pair)
    positions = jnp.arange(sec_size, dtype=jnp.int32)
    row_mask = (positions < small_lookup(left_live, sector) * BLOCK).astype(jnp.float32)
    col_mask = (positions < small_lookup(right_live, sector + own_step) * BLOCK).astype(jnp.float32)
    live = row_mask[:, None] * col_mask[None, :]
    entries = float(state.shape[0] * sec_size * sec_size * lax.axis_size(AXES))

    masked = state[0] * live
    rows = sec_size // CHUNKS
    spread = masked_square_sum(pairs, block_index.astype(jnp.int32), left_live, right_live, state)
    spread, head = lax.optimization_barrier((spread, masked[:rows]))
    head_far = shift_up(head, 2)
    start_sum = exchange_sum(spread)[0, 0]
    start_mean = start_sum / entries
    scale = jnp.sqrt(start_mean + 1e-06)
    vector = masked / scale
    pieces = [
        row_major((masked[c * rows:(c + 1) * rows] / scale).astype(jnp.bfloat16))
        for c in range(CHUNKS)
    ]
    head_two = row_major((head_far / scale).astype(jnp.bfloat16))
    rounded = jnp.concatenate(pieces, axis=0)

    weights = []
    for offset in (2, 3):
        source_pair = (own_pair - offset) % pairs
        valid = block_index >= offset
        weights.append(
            jnp.where(
                valid, table_entry(site_ops[0], own_pair, source_pair), jnp.zeros((), jnp.float32)
            )
        )

    part_one = jnp.dot(rounded, right_env[1, 0], preferred_element_type=jnp.float32).astype(
        jnp.bfloat16
    )
    diag_weight = table_entry(site_ops[1], own_pair, own_pair)
    image_one = diag_weight * jnp.dot(left_env[1, 0], part_one, preferred_element_type=jnp.float32)

    image_one, pieces[-1] = lax.optimization_barrier((image_one, pieces[-1]))
    parts = []
    for c in range(CHUNKS):
        far_two = head_two if c == 0 else shift_up(pieces[c], 2)
        far_three = shift_up(far_two, 1)
        source = (
            weights[0] * far_two.astype(jnp.float32) + weights[1] * far_three.astype(jnp.float32)
        ).astype(jnp.bfloat16)
        parts.append(
            jnp.dot(source, right_env[0, 0], preferred_element_type=jnp.float32).astype(jnp.bfloat16)
        )
    part_zero = jnp.concatenate(parts, axis=0)
    image = jnp.dot(left_env[0, 0], part_zero, preferred_element_type=jnp.float32) + image_one
    image = row_major(image * live)

    sums = all_sum(jnp.sum(jnp.stack([vector * image, image * image]), axis=(1, 2)))
    alpha_value = sums[0:1] / entries
    vector_mean = start_mean / (start_mean + 1e-06)
    residual_mean = sums[1:2] / entries - alpha_value * alpha_value * (2.0 - vector_mean)
    beta_value = jnp.sqrt(residual_mean + 1e-06)
    residual = image - alpha_value[:, None] * vector
    next_vector = residual / beta_value[:, None]
    return (next_vector[None], jnp.concatenate([alpha_value, beta_value]))


def solution(mesh):
    in_specs = (
        P(AXES, None, None),
        P(None, AXES, None, None),
        P(None, AXES, None, None),
        P(),
        P(),
        P(),
    )
    out_specs = (P(AXES, None, None), P())
    return jax.shard_map(
        per_device, mesh=mesh, in_specs=in_specs, out_specs=out_specs, check_vma=False
    )
```

```python
import functools

import jax
import jax.numpy as jnp
from jax import lax
from jax.sharding import PartitionSpec as P
from jax.experimental.layout import Layout, with_layout_constraint
from jax.experimental import pallas as pl
from jax.experimental.pallas import tpu as pltpu

BLOCK = 256
AXES = ("left", "right")
CHUNKS = 4


def shift_up(block, distance):
    devices = range(lax.axis_size(AXES))
    route = [(i - distance, i) for i in devices if i - distance in devices]
    return lax.ppermute(block, AXES, route)


def all_sum(values):
    count = lax.axis_size(AXES)
    return exchange_sum(jnp.broadcast_to(values[None], (count,) + values.shape))


def exchange_sum(spread):
    return jnp.sum(lax.all_to_all(spread, AXES, 0, 0, tiled=True), axis=0)


def square_sum_kernel(pairs, index_ref, left_ref, right_ref, state_ref, out_ref, acc_ref):
    step = pl.program_id(0)
    rows, cols = state_ref.shape[1], state_ref.shape[2]
    sector = index_ref[0] // pairs
    pair = index_ref[0] % pairs
    row_limit = left_ref[sector] * BLOCK
    col_limit = right_ref[sector + (pair + 1) // 2] * BLOCK

    @pl.when(step == 0)
    def _():
        acc_ref[...] = jnp.zeros_like(acc_ref)

    x = state_ref[0]
    row_ids = step * rows + lax.broadcasted_iota(jnp.int32, (rows, cols), 0)
    col_ids = lax.broadcasted_iota(jnp.int32, (rows, cols), 1)
    x = jnp.where((row_ids < row_limit) & (col_ids < col_limit), x, 0.0)
    acc_ref[...] += jnp.sum((x * x).reshape(rows // 8, 8, cols), axis=0)

    @pl.when(step == pl.num_programs(0) - 1)
    def _():
        out_ref[...] = jnp.full(out_ref.shape, jnp.sum(acc_ref[...]), jnp.float32)


def masked_square_sum(pairs, block_index, left_live, right_live, state):
    count = lax.axis_size(AXES)
    sec_size = state.shape[1]
    rows = 256
    return pl.pallas_call(
        functools.partial(square_sum_kernel, pairs),
        grid_spec=pltpu.PrefetchScalarGridSpec(
            num_scalar_prefetch=3,
            grid=(sec_size // rows,),
            in_specs=[pl.BlockSpec((1, rows, sec_size), lambda i, *_: (0, i, 0))],
            out_specs=pl.BlockSpec((count, 1, 1), lambda i, *_: (0, 0, 0)),
            scratch_shapes=[pltpu.VMEM((8, sec_size), jnp.float32)],
        ),
        out_shape=jax.ShapeDtypeStruct((count, 1, 1), jnp.float32),
    )(block_index.reshape(1), left_live, right_live, state)


def row_major(array):
    return with_layout_constraint(array, Layout(major_to_minor=tuple(range(array.ndim))))


def small_lookup(table, index):
    return lax.dynamic_index_in_dim(table, index, 0, keepdims=False)


def table_entry(table, row, column):
    return small_lookup(small_lookup(table, row), column)


def per_device(state, left_env, right_env, site_ops, left_live, right_live):
    pairs = site_ops.shape[1]
    sec_size = state.shape[1]
    block_index = lax.axis_index("left") * lax.axis_size("right") + lax.axis_index("right")
    own_pair = block_index % pairs
    sector = block_index // pairs
    steps = (jnp.arange(pairs, dtype=jnp.int32) + 1) // 2
    own_step = small_lookup(steps, own_pair)
    positions = jnp.arange(sec_size, dtype=jnp.int32)
    row_mask = (positions < small_lookup(left_live, sector) * BLOCK).astype(jnp.float32)
    col_mask = (positions < small_lookup(right_live, sector + own_step) * BLOCK).astype(jnp.float32)
    live = row_mask[:, None] * col_mask[None, :]
    entries = float(state.shape[0] * sec_size * sec_size * lax.axis_size(AXES))

    masked = state[0] * live
    rows = sec_size // CHUNKS
    spread = masked_square_sum(pairs, block_index.astype(jnp.int32), left_live, right_live, state)
    spread, head = lax.optimization_barrier((spread, masked[:rows]))
    head_far = shift_up(head, 2)
    start_sum = exchange_sum(spread)[0, 0]
    start_mean = start_sum / entries
    scale = jnp.sqrt(start_mean + 1e-06)
    vector = masked / scale
    pieces = [
        row_major((masked[c * rows:(c + 1) * rows] / scale).astype(jnp.bfloat16))
        for c in range(CHUNKS)
    ]
    head_two = row_major((head_far / scale).astype(jnp.bfloat16))
    head_two, pieces[1] = lax.optimization_barrier((head_two, pieces[1]))
    rounded = jnp.concatenate(pieces, axis=0)

    weights = []
    for offset in (2, 3):
        source_pair = (own_pair - offset) % pairs
        valid = block_index >= offset
        weights.append(
            jnp.where(
                valid, table_entry(site_ops[0], own_pair, source_pair), jnp.zeros((), jnp.float32)
            )
        )

    part_one = jnp.dot(rounded, right_env[1, 0], preferred_element_type=jnp.float32).astype(
        jnp.bfloat16
    )
    diag_weight = table_entry(site_ops[1], own_pair, own_pair)
    image_one = diag_weight * jnp.dot(left_env[1, 0], part_one, preferred_element_type=jnp.float32)

    image_one, pieces[-1] = lax.optimization_barrier((image_one, pieces[-1]))
    parts = []
    for c in range(CHUNKS):
        far_two = head_two if c == 0 else shift_up(pieces[c], 2)
        far_three = shift_up(far_two, 1)
        source = (
            weights[0] * far_two.astype(jnp.float32) + weights[1] * far_three.astype(jnp.float32)
        ).astype(jnp.bfloat16)
        parts.append(
            jnp.dot(source, right_env[0, 0], preferred_element_type=jnp.float32).astype(jnp.bfloat16)
        )
    part_zero = jnp.concatenate(parts, axis=0)
    image = jnp.dot(left_env[0, 0], part_zero, preferred_element_type=jnp.float32) + image_one
    image = row_major(image * live)

    sums = all_sum(jnp.sum(jnp.stack([vector * image, image * image]), axis=(1, 2)))
    alpha_value = sums[0:1] / entries
    vector_mean = start_mean / (start_mean + 1e-06)
    residual_mean = sums[1:2] / entries - alpha_value * alpha_value * (2.0 - vector_mean)
    beta_value = jnp.sqrt(residual_mean + 1e-06)
    residual = image - alpha_value[:, None] * vector
    next_vector = residual / beta_value[:, None]
    return (next_vector[None], jnp.concatenate([alpha_value, beta_value]))


def solution(mesh):
    in_specs = (
        P(AXES, None, None),
        P(None, AXES, None, None),
        P(None, AXES, None, None),
        P(),
        P(),
        P(),
    )
    out_specs = (P(AXES, None, None), P())
    return jax.shard_map(
        per_device, mesh=mesh, in_specs=in_specs, out_specs=out_specs, check_vma=False
    )
```

```python
import functools

import jax
import jax.numpy as jnp
from jax import lax
from jax.sharding import PartitionSpec as P
from jax.experimental.layout import Layout, with_layout_constraint
from jax.experimental import pallas as pl
from jax.experimental.pallas import tpu as pltpu

BLOCK = 256
AXES = ("left", "right")
CHUNKS = 8


def shift_up(block, distance):
    devices = range(lax.axis_size(AXES))
    route = [(i - distance, i) for i in devices if i - distance in devices]
    return lax.ppermute(block, AXES, route)


def all_sum(values):
    count = lax.axis_size(AXES)
    return exchange_sum(jnp.broadcast_to(values[None], (count,) + values.shape))


def exchange_sum(spread):
    return jnp.sum(lax.all_to_all(spread, AXES, 0, 0, tiled=True), axis=0)


def square_sum_kernel(pairs, index_ref, left_ref, right_ref, state_ref, out_ref, acc_ref):
    step = pl.program_id(0)
    rows, cols = state_ref.shape[1], state_ref.shape[2]
    sector = index_ref[0] // pairs
    pair = index_ref[0] % pairs
    row_limit = left_ref[sector] * BLOCK
    col_limit = right_ref[sector + (pair + 1) // 2] * BLOCK

    @pl.when(step == 0)
    def _():
        acc_ref[...] = jnp.zeros_like(acc_ref)

    x = state_ref[0]
    row_ids = step * rows + lax.broadcasted_iota(jnp.int32, (rows, cols), 0)
    col_ids = lax.broadcasted_iota(jnp.int32, (rows, cols), 1)
    x = jnp.where((row_ids < row_limit) & (col_ids < col_limit), x, 0.0)
    acc_ref[...] += jnp.sum((x * x).reshape(rows // 8, 8, cols), axis=0)

    @pl.when(step == pl.num_programs(0) - 1)
    def _():
        out_ref[...] = jnp.full(out_ref.shape, jnp.sum(acc_ref[...]), jnp.float32)


def masked_square_sum(pairs, block_index, left_live, right_live, state):
    count = lax.axis_size(AXES)
    sec_size = state.shape[1]
    rows = 256
    return pl.pallas_call(
        functools.partial(square_sum_kernel, pairs),
        grid_spec=pltpu.PrefetchScalarGridSpec(
            num_scalar_prefetch=3,
            grid=(sec_size // rows,),
            in_specs=[pl.BlockSpec((1, rows, sec_size), lambda i, *_: (0, i, 0))],
            out_specs=pl.BlockSpec((count, 1, 1), lambda i, *_: (0, 0, 0)),
            scratch_shapes=[pltpu.VMEM((8, sec_size), jnp.float32)],
        ),
        out_shape=jax.ShapeDtypeStruct((count, 1, 1), jnp.float32),
    )(block_index.reshape(1), left_live, right_live, state)


def row_major(array):
    return with_layout_constraint(array, Layout(major_to_minor=tuple(range(array.ndim))))


def small_lookup(table, index):
    return lax.dynamic_index_in_dim(table, index, 0, keepdims=False)


def table_entry(table, row, column):
    return small_lookup(small_lookup(table, row), column)


def per_device(state, left_env, right_env, site_ops, left_live, right_live):
    pairs = site_ops.shape[1]
    sec_size = state.shape[1]
    block_index = lax.axis_index("left") * lax.axis_size("right") + lax.axis_index("right")
    own_pair = block_index % pairs
    sector = block_index // pairs
    steps = (jnp.arange(pairs, dtype=jnp.int32) + 1) // 2
    own_step = small_lookup(steps, own_pair)
    positions = jnp.arange(sec_size, dtype=jnp.int32)
    row_mask = (positions < small_lookup(left_live, sector) * BLOCK).astype(jnp.float32)
    col_mask = (positions < small_lookup(right_live, sector + own_step) * BLOCK).astype(jnp.float32)
    live = row_mask[:, None] * col_mask[None, :]
    entries = float(state.shape[0] * sec_size * sec_size * lax.axis_size(AXES))

    masked = state[0] * live
    start_sum = exchange_sum(
        masked_square_sum(pairs, block_index.astype(jnp.int32), left_live, right_live, state)
    )[0, 0]
    start_mean = start_sum / entries
    scale = jnp.sqrt(start_mean + 1e-06)
    vector = masked / scale
    rows = sec_size // CHUNKS
    pieces = [
        row_major((masked[c * rows:(c + 1) * rows] / scale).astype(jnp.bfloat16))
        for c in range(CHUNKS)
    ]
    rounded = jnp.concatenate(pieces, axis=0)

    weights = []
    for offset in (2, 3):
        source_pair = (own_pair - offset) % pairs
        valid = block_index >= offset
        weights.append(
            jnp.where(
                valid, table_entry(site_ops[0], own_pair, source_pair), jnp.zeros((), jnp.float32)
            )
        )

    part_one = jnp.dot(rounded, right_env[1, 0], preferred_element_type=jnp.float32).astype(
        jnp.bfloat16
    )
    diag_weight = table_entry(site_ops[1], own_pair, own_pair)
    image_one = diag_weight * jnp.dot(left_env[1, 0], part_one, preferred_element_type=jnp.float32)

    image_one, pieces[-1] = lax.optimization_barrier((image_one, pieces[-1]))
    parts = []
    for c in range(CHUNKS):
        far_two = shift_up(pieces[c], 2)
        far_three = shift_up(far_two, 1)
        source = (
            weights[0] * far_two.astype(jnp.float32) + weights[1] * far_three.astype(jnp.float32)
        ).astype(jnp.bfloat16)
        parts.append(
            jnp.dot(source, right_env[0, 0], preferred_element_type=jnp.float32).astype(jnp.bfloat16)
        )
    part_zero = jnp.concatenate(parts, axis=0)
    image = jnp.dot(left_env[0, 0], part_zero, preferred_element_type=jnp.float32) + image_one
    image = row_major(image * live)

    sums = all_sum(jnp.sum(jnp.stack([vector * image, image * image]), axis=(1, 2)))
    alpha_value = sums[0:1] / entries
    vector_mean = start_mean / (start_mean + 1e-06)
    residual_mean = sums[1:2] / entries - alpha_value * alpha_value * (2.0 - vector_mean)
    beta_value = jnp.sqrt(residual_mean + 1e-06)
    residual = image - alpha_value[:, None] * vector
    next_vector = residual / beta_value[:, None]
    return (next_vector[None], jnp.concatenate([alpha_value, beta_value]))


def solution(mesh):
    in_specs = (
        P(AXES, None, None),
        P(None, AXES, None, None),
        P(None, AXES, None, None),
        P(),
        P(),
        P(),
    )
    out_specs = (P(AXES, None, None), P())
    return jax.shard_map(
        per_device, mesh=mesh, in_specs=in_specs, out_specs=out_specs, check_vma=False
    )
```

```python
import functools

import jax
import jax.numpy as jnp
from jax import lax
from jax.sharding import PartitionSpec as P
from jax.experimental.layout import Layout, with_layout_constraint
from jax.experimental import pallas as pl
from jax.experimental.pallas import tpu as pltpu

BLOCK = 256
AXES = ("left", "right")
CHUNKS = 2


def shift_up(block, distance):
    devices = range(lax.axis_size(AXES))
    route = [(i - distance, i) for i in devices if i - distance in devices]
    return lax.ppermute(block, AXES, route)


def all_sum(values):
    count = lax.axis_size(AXES)
    return exchange_sum(jnp.broadcast_to(values[None], (count,) + values.shape))


def exchange_sum(spread):
    return jnp.sum(lax.all_to_all(spread, AXES, 0, 0, tiled=True), axis=0)


def square_sum_kernel(pairs, index_ref, left_ref, right_ref, state_ref, out_ref, acc_ref):
    step = pl.program_id(0)
    rows, cols = state_ref.shape[1], state_ref.shape[2]
    sector = index_ref[0] // pairs
    pair = index_ref[0] % pairs
    row_limit = left_ref[sector] * BLOCK
    col_limit = right_ref[sector + (pair + 1) // 2] * BLOCK

    @pl.when(step == 0)
    def _():
        acc_ref[...] = jnp.zeros_like(acc_ref)

    x = state_ref[0]
    row_ids = step * rows + lax.broadcasted_iota(jnp.int32, (rows, cols), 0)
    col_ids = lax.broadcasted_iota(jnp.int32, (rows, cols), 1)
    x = jnp.where((row_ids < row_limit) & (col_ids < col_limit), x, 0.0)
    acc_ref[...] += jnp.sum((x * x).reshape(rows // 8, 8, cols), axis=0)

    @pl.when(step == pl.num_programs(0) - 1)
    def _():
        out_ref[...] = jnp.full(out_ref.shape, jnp.sum(acc_ref[...]), jnp.float32)


def masked_square_sum(pairs, block_index, left_live, right_live, state):
    count = lax.axis_size(AXES)
    sec_size = state.shape[1]
    rows = 256
    return pl.pallas_call(
        functools.partial(square_sum_kernel, pairs),
        grid_spec=pltpu.PrefetchScalarGridSpec(
            num_scalar_prefetch=3,
            grid=(sec_size // rows,),
            in_specs=[pl.BlockSpec((1, rows, sec_size), lambda i, *_: (0, i, 0))],
            out_specs=pl.BlockSpec((count, 1, 1), lambda i, *_: (0, 0, 0)),
            scratch_shapes=[pltpu.VMEM((8, sec_size), jnp.float32)],
        ),
        out_shape=jax.ShapeDtypeStruct((count, 1, 1), jnp.float32),
    )(block_index.reshape(1), left_live, right_live, state)


def row_major(array):
    return with_layout_constraint(array, Layout(major_to_minor=tuple(range(array.ndim))))


def small_lookup(table, index):
    return lax.dynamic_index_in_dim(table, index, 0, keepdims=False)


def table_entry(table, row, column):
    return small_lookup(small_lookup(table, row), column)


def per_device(state, left_env, right_env, site_ops, left_live, right_live):
    pairs = site_ops.shape[1]
    sec_size = state.shape[1]
    block_index = lax.axis_index("left") * lax.axis_size("right") + lax.axis_index("right")
    own_pair = block_index % pairs
    sector = block_index // pairs
    steps = (jnp.arange(pairs, dtype=jnp.int32) + 1) // 2
    own_step = small_lookup(steps, own_pair)
    positions = jnp.arange(sec_size, dtype=jnp.int32)
    row_mask = (positions < small_lookup(left_live, sector) * BLOCK).astype(jnp.float32)
    col_mask = (positions < small_lookup(right_live, sector + own_step) * BLOCK).astype(jnp.float32)
    live = row_mask[:, None] * col_mask[None, :]
    entries = float(state.shape[0] * sec_size * sec_size * lax.axis_size(AXES))

    masked = state[0] * live
    start_sum = exchange_sum(
        masked_square_sum(pairs, block_index.astype(jnp.int32), left_live, right_live, state)
    )[0, 0]
    start_mean = start_sum / entries
    scale = jnp.sqrt(start_mean + 1e-06)
    vector = masked / scale
    rows = sec_size // CHUNKS
    pieces = [
        row_major((masked[c * rows:(c + 1) * rows] / scale).astype(jnp.bfloat16))
        for c in range(CHUNKS)
    ]
    rounded = jnp.concatenate(pieces, axis=0)

    weights = []
    for offset in (2, 3):
        source_pair = (own_pair - offset) % pairs
        valid = block_index >= offset
        weights.append(
            jnp.where(
                valid, table_entry(site_ops[0], own_pair, source_pair), jnp.zeros((), jnp.float32)
            )
        )

    part_one = jnp.dot(rounded, right_env[1, 0], preferred_element_type=jnp.float32).astype(
        jnp.bfloat16
    )
    diag_weight = table_entry(site_ops[1], own_pair, own_pair)
    image_one = diag_weight * jnp.dot(left_env[1, 0], part_one, preferred_element_type=jnp.float32)

    image_one, pieces[-1] = lax.optimization_barrier((image_one, pieces[-1]))
    parts = []
    for c in range(CHUNKS):
        far_two = shift_up(pieces[c], 2)
        far_three = shift_up(far_two, 1)
        source = (
            weights[0] * far_two.astype(jnp.float32) + weights[1] * far_three.astype(jnp.float32)
        ).astype(jnp.bfloat16)
        parts.append(
            jnp.dot(source, right_env[0, 0], preferred_element_type=jnp.float32).astype(jnp.bfloat16)
        )
    part_zero = jnp.concatenate(parts, axis=0)
    image = jnp.dot(left_env[0, 0], part_zero, preferred_element_type=jnp.float32) + image_one
    image = row_major(image * live)

    sums = all_sum(jnp.sum(jnp.stack([vector * image, image * image]), axis=(1, 2)))
    alpha_value = sums[0:1] / entries
    vector_mean = start_mean / (start_mean + 1e-06)
    residual_mean = sums[1:2] / entries - alpha_value * alpha_value * (2.0 - vector_mean)
    beta_value = jnp.sqrt(residual_mean + 1e-06)
    residual = image - alpha_value[:, None] * vector
    next_vector = residual / beta_value[:, None]
    return (next_vector[None], jnp.concatenate([alpha_value, beta_value]))


def solution(mesh):
    in_specs = (
        P(AXES, None, None),
        P(None, AXES, None, None),
        P(None, AXES, None, None),
        P(),
        P(),
        P(),
    )
    out_specs = (P(AXES, None, None), P())
    return jax.shard_map(
        per_device, mesh=mesh, in_specs=in_specs, out_specs=out_specs, check_vma=False
    )
```

```python
import functools

import jax
import jax.numpy as jnp
from jax import lax
from jax.sharding import PartitionSpec as P
from jax.experimental.layout import Layout, with_layout_constraint
from jax.experimental import pallas as pl
from jax.experimental.pallas import tpu as pltpu

BLOCK = 256
AXES = ("left", "right")
CHUNKS = 4


def shift_up(block, distance):
    devices = range(lax.axis_size(AXES))
    route = [(i - distance, i) for i in devices if i - distance in devices]
    return lax.ppermute(block, AXES, route)


def all_sum(values):
    count = lax.axis_size(AXES)
    return exchange_sum(jnp.broadcast_to(values[None], (count,) + values.shape))


def exchange_sum(spread):
    return jnp.sum(lax.all_to_all(spread, AXES, 0, 0, tiled=True), axis=0)


def square_sum_kernel(pairs, index_ref, left_ref, right_ref, state_ref, out_ref, acc_ref):
    step = pl.program_id(0)
    rows, cols = state_ref.shape[1], state_ref.shape[2]
    sector = index_ref[0] // pairs
    pair = index_ref[0] % pairs
    row_limit = left_ref[sector] * BLOCK
    col_limit = right_ref[sector + (pair + 1) // 2] * BLOCK

    @pl.when(step == 0)
    def _():
        acc_ref[...] = jnp.zeros_like(acc_ref)

    x = state_ref[0]
    row_ids = step * rows + lax.broadcasted_iota(jnp.int32, (rows, cols), 0)
    col_ids = lax.broadcasted_iota(jnp.int32, (rows, cols), 1)
    x = jnp.where((row_ids < row_limit) & (col_ids < col_limit), x, 0.0)
    acc_ref[...] += jnp.sum((x * x).reshape(rows // 8, 8, cols), axis=0)

    @pl.when(step == pl.num_programs(0) - 1)
    def _():
        out_ref[...] = jnp.full(out_ref.shape, jnp.sum(acc_ref[...]), jnp.float32)


def masked_square_sum(pairs, block_index, left_live, right_live, state):
    count = lax.axis_size(AXES)
    sec_size = state.shape[1]
    rows = 256
    return pl.pallas_call(
        functools.partial(square_sum_kernel, pairs),
        grid_spec=pltpu.PrefetchScalarGridSpec(
            num_scalar_prefetch=3,
            grid=(sec_size // rows,),
            in_specs=[pl.BlockSpec((1, rows, sec_size), lambda i, *_: (0, i, 0))],
            out_specs=pl.BlockSpec((count, 1, 1), lambda i, *_: (0, 0, 0)),
            scratch_shapes=[pltpu.VMEM((8, sec_size), jnp.float32)],
        ),
        out_shape=jax.ShapeDtypeStruct((count, 1, 1), jnp.float32),
    )(block_index.reshape(1), left_live, right_live, state)


def row_major(array):
    return with_layout_constraint(array, Layout(major_to_minor=tuple(range(array.ndim))))


def small_lookup(table, index):
    return lax.dynamic_index_in_dim(table, index, 0, keepdims=False)


def table_entry(table, row, column):
    return small_lookup(small_lookup(table, row), column)


def per_device(state, left_env, right_env, site_ops, left_live, right_live):
    pairs = site_ops.shape[1]
    sec_size = state.shape[1]
    block_index = lax.axis_index("left") * lax.axis_size("right") + lax.axis_index("right")
    own_pair = block_index % pairs
    sector = block_index // pairs
    steps = (jnp.arange(pairs, dtype=jnp.int32) + 1) // 2
    own_step = small_lookup(steps, own_pair)
    positions = jnp.arange(sec_size, dtype=jnp.int32)
    row_mask = (positions < small_lookup(left_live, sector) * BLOCK).astype(jnp.float32)
    col_mask = (positions < small_lookup(right_live, sector + own_step) * BLOCK).astype(jnp.float32)
    live = row_mask[:, None] * col_mask[None, :]
    entries = float(state.shape[0] * sec_size * sec_size * lax.axis_size(AXES))

    masked = state[0] * live
    start_sum = exchange_sum(
        masked_square_sum(pairs, block_index.astype(jnp.int32), left_live, right_live, state)
    )[0, 0]
    start_mean = start_sum / entries
    scale = jnp.sqrt(start_mean + 1e-06)
    vector = masked / scale
    rows = sec_size // CHUNKS
    pieces = [
        row_major((masked[c * rows:(c + 1) * rows] / scale).astype(jnp.bfloat16))
        for c in range(CHUNKS)
    ]
    rounded = jnp.concatenate(pieces, axis=0)

    weights = []
    for offset in (2, 3):
        source_pair = (own_pair - offset) % pairs
        valid = block_index >= offset
        weights.append(
            jnp.where(
                valid, table_entry(site_ops[0], own_pair, source_pair), jnp.zeros((), jnp.float32)
            )
        )

    part_one = jnp.dot(rounded, right_env[1, 0], preferred_element_type=jnp.float32).astype(
        jnp.bfloat16
    )
    diag_weight = table_entry(site_ops[1], own_pair, own_pair)
    image_one = diag_weight * jnp.dot(left_env[1, 0], part_one, preferred_element_type=jnp.float32)

    parts = []
    for c in range(CHUNKS):
        far_two = shift_up(pieces[c], 2)
        if c == 0:
            image_one, far_two = lax.optimization_barrier((image_one, far_two))
        far_three = shift_up(far_two, 1)
        source = (
            weights[0] * far_two.astype(jnp.float32) + weights[1] * far_three.astype(jnp.float32)
        ).astype(jnp.bfloat16)
        parts.append(
            jnp.dot(source, right_env[0, 0], preferred_element_type=jnp.float32).astype(jnp.bfloat16)
        )
    part_zero = jnp.concatenate(parts, axis=0)
    image = jnp.dot(left_env[0, 0], part_zero, preferred_element_type=jnp.float32) + image_one
    image = row_major(image * live)

    sums = all_sum(jnp.sum(jnp.stack([vector * image, image * image]), axis=(1, 2)))
    alpha_value = sums[0:1] / entries
    vector_mean = start_mean / (start_mean + 1e-06)
    residual_mean = sums[1:2] / entries - alpha_value * alpha_value * (2.0 - vector_mean)
    beta_value = jnp.sqrt(residual_mean + 1e-06)
    residual = image - alpha_value[:, None] * vector
    next_vector = residual / beta_value[:, None]
    return (next_vector[None], jnp.concatenate([alpha_value, beta_value]))


def solution(mesh):
    in_specs = (
        P(AXES, None, None),
        P(None, AXES, None, None),
        P(None, AXES, None, None),
        P(),
        P(),
        P(),
    )
    out_specs = (P(AXES, None, None), P())
    return jax.shard_map(
        per_device, mesh=mesh, in_specs=in_specs, out_specs=out_specs, check_vma=False
    )
```

```python
import functools

import jax
import jax.numpy as jnp
from jax import lax
from jax.sharding import PartitionSpec as P
from jax.experimental.layout import Layout, with_layout_constraint
from jax.experimental import pallas as pl
from jax.experimental.pallas import tpu as pltpu

BLOCK = 256
AXES = ("left", "right")
CHUNKS = 4


def shift_up(block, distance):
    devices = range(lax.axis_size(AXES))
    route = [(i - distance, i) for i in devices if i - distance in devices]
    return lax.ppermute(block, AXES, route)


def all_sum(values):
    count = lax.axis_size(AXES)
    return exchange_sum(jnp.broadcast_to(values[None], (count,) + values.shape))


def exchange_sum(spread):
    return jnp.sum(lax.all_to_all(spread, AXES, 0, 0, tiled=True), axis=0)


def square_sum_kernel(pairs, index_ref, left_ref, right_ref, state_ref, out_ref, acc_ref):
    step = pl.program_id(0)
    rows, cols = state_ref.shape[1], state_ref.shape[2]
    sector = index_ref[0] // pairs
    pair = index_ref[0] % pairs
    row_limit = left_ref[sector] * BLOCK
    col_limit = right_ref[sector + (pair + 1) // 2] * BLOCK

    @pl.when(step == 0)
    def _():
        acc_ref[...] = jnp.zeros_like(acc_ref)

    x = state_ref[0]
    row_ids = step * rows + lax.broadcasted_iota(jnp.int32, (rows, cols), 0)
    col_ids = lax.broadcasted_iota(jnp.int32, (rows, cols), 1)
    x = jnp.where((row_ids < row_limit) & (col_ids < col_limit), x, 0.0)
    acc_ref[...] += jnp.sum((x * x).reshape(rows // 8, 8, cols), axis=0)

    @pl.when(step == pl.num_programs(0) - 1)
    def _():
        out_ref[...] = jnp.full(out_ref.shape, jnp.sum(acc_ref[...]), jnp.float32)


def masked_square_sum(pairs, block_index, left_live, right_live, state):
    count = lax.axis_size(AXES)
    sec_size = state.shape[1]
    rows = 256
    return pl.pallas_call(
        functools.partial(square_sum_kernel, pairs),
        grid_spec=pltpu.PrefetchScalarGridSpec(
            num_scalar_prefetch=3,
            grid=(sec_size // rows,),
            in_specs=[pl.BlockSpec((1, rows, sec_size), lambda i, *_: (0, i, 0))],
            out_specs=pl.BlockSpec((count, 1, 1), lambda i, *_: (0, 0, 0)),
            scratch_shapes=[pltpu.VMEM((8, sec_size), jnp.float32)],
        ),
        out_shape=jax.ShapeDtypeStruct((count, 1, 1), jnp.float32),
    )(block_index.reshape(1), left_live, right_live, state)


def row_major(array):
    return with_layout_constraint(array, Layout(major_to_minor=tuple(range(array.ndim))))


def small_lookup(table, index):
    return lax.dynamic_index_in_dim(table, index, 0, keepdims=False)


def table_entry(table, row, column):
    return small_lookup(small_lookup(table, row), column)


def per_device(state, left_env, right_env, site_ops, left_live, right_live):
    pairs = site_ops.shape[1]
    sec_size = state.shape[1]
    block_index = lax.axis_index("left") * lax.axis_size("right") + lax.axis_index("right")
    own_pair = block_index % pairs
    sector = block_index // pairs
    steps = (jnp.arange(pairs, dtype=jnp.int32) + 1) // 2
    own_step = small_lookup(steps, own_pair)
    positions = jnp.arange(sec_size, dtype=jnp.int32)
    row_mask = (positions < small_lookup(left_live, sector) * BLOCK).astype(jnp.float32)
    col_mask = (positions < small_lookup(right_live, sector + own_step) * BLOCK).astype(jnp.float32)
    live = row_mask[:, None] * col_mask[None, :]
    entries = float(state.shape[0] * sec_size * sec_size * lax.axis_size(AXES))

    masked = state[0] * live
    start_sum = exchange_sum(
        masked_square_sum(pairs, block_index.astype(jnp.int32), left_live, right_live, state)
    )[0, 0]
    start_mean = start_sum / entries
    scale = jnp.sqrt(start_mean + 1e-06)
    vector = masked / scale
    rows = sec_size // CHUNKS
    pieces = [
        row_major((masked[c * rows:(c + 1) * rows] / scale).astype(jnp.bfloat16))
        for c in range(CHUNKS)
    ]
    rounded = jnp.concatenate(pieces, axis=0)

    weights = []
    for offset in (2, 3):
        source_pair = (own_pair - offset) % pairs
        valid = block_index >= offset
        weights.append(
            jnp.where(
                valid, table_entry(site_ops[0], own_pair, source_pair), jnp.zeros((), jnp.float32)
            )
        )

    part_one = jnp.dot(rounded, right_env[1, 0], preferred_element_type=jnp.float32).astype(
        jnp.bfloat16
    )
    diag_weight = table_entry(site_ops[1], own_pair, own_pair)
    image_one = diag_weight * jnp.dot(left_env[1, 0], part_one, preferred_element_type=jnp.float32)

    image_one, pieces[-1] = lax.optimization_barrier((image_one, pieces[-1]))
    parts = []
    for c in range(CHUNKS):
        far_two = shift_up(pieces[c], 2)
        far_three = shift_up(far_two, 1)
        source = (
            weights[0] * far_two.astype(jnp.float32) + weights[1] * far_three.astype(jnp.float32)
        ).astype(jnp.bfloat16)
        parts.append(
            jnp.dot(source, right_env[0, 0], preferred_element_type=jnp.float32).astype(jnp.bfloat16)
        )
    part_zero = jnp.concatenate(parts, axis=0)
    image = jnp.dot(left_env[0, 0], part_zero, preferred_element_type=jnp.float32) + image_one
    image = row_major(image * live)

    sums = all_sum(jnp.sum(jnp.stack([vector * image, image * image]), axis=(1, 2)))
    vector_mean = start_mean / (start_mean + 1e-06)
    means = sums / entries
    swapped = means[::-1]
    lane = lax.broadcasted_iota(jnp.int32, means.shape, 0)
    coefficients = jnp.where(
        lane == 0, means, jnp.sqrt(means - swapped * swapped * (2.0 - vector_mean) + 1e-06)
    )
    residual = image - coefficients[0] * vector
    next_vector = residual / coefficients[1]
    return (next_vector[None], coefficients)


def solution(mesh):
    in_specs = (
        P(AXES, None, None),
        P(None, AXES, None, None),
        P(None, AXES, None, None),
        P(),
        P(),
        P(),
    )
    out_specs = (P(AXES, None, None), P())
    return jax.shard_map(
        per_device, mesh=mesh, in_specs=in_specs, out_specs=out_specs, check_vma=False
    )
```

```python
import functools

import jax
import jax.numpy as jnp
from jax import lax
from jax.sharding import PartitionSpec as P
from jax.experimental.layout import Layout, with_layout_constraint
from jax.experimental import pallas as pl
from jax.experimental.pallas import tpu as pltpu

BLOCK = 256
AXES = ("left", "right")
CHUNKS = 4


def shift_up(block, distance):
    devices = range(lax.axis_size(AXES))
    route = [(i - distance, i) for i in devices if i - distance in devices]
    return lax.ppermute(block, AXES, route)


def all_sum(values):
    count = lax.axis_size(AXES)
    return exchange_sum(jnp.broadcast_to(values[None], (count,) + values.shape))


def exchange_sum(spread):
    return jnp.sum(lax.all_to_all(spread, AXES, 0, 0, tiled=True), axis=0)


def square_sum_kernel(pairs, index_ref, left_ref, right_ref, state_ref, out_ref, acc_ref):
    step = pl.program_id(0)
    rows, cols = state_ref.shape[1], state_ref.shape[2]
    sector = index_ref[0] // pairs
    pair = index_ref[0] % pairs
    row_limit = left_ref[sector] * BLOCK
    col_limit = right_ref[sector + (pair + 1) // 2] * BLOCK

    @pl.when(step == 0)
    def _():
        acc_ref[...] = jnp.zeros_like(acc_ref)

    x = state_ref[0]
    row_ids = step * rows + lax.broadcasted_iota(jnp.int32, (rows, cols), 0)
    col_ids = lax.broadcasted_iota(jnp.int32, (rows, cols), 1)
    x = jnp.where((row_ids < row_limit) & (col_ids < col_limit), x, 0.0)
    acc_ref[...] += jnp.sum((x * x).reshape(rows // 8, 8, cols), axis=0)

    @pl.when(step == pl.num_programs(0) - 1)
    def _():
        out_ref[...] = jnp.full(out_ref.shape, jnp.sum(acc_ref[...]), jnp.float32)


def masked_square_sum(pairs, block_index, left_live, right_live, state):
    count = lax.axis_size(AXES)
    sec_size = state.shape[1]
    rows = 256
    return pl.pallas_call(
        functools.partial(square_sum_kernel, pairs),
        grid_spec=pltpu.PrefetchScalarGridSpec(
            num_scalar_prefetch=3,
            grid=(sec_size // rows,),
            in_specs=[pl.BlockSpec((1, rows, sec_size), lambda i, *_: (0, i, 0))],
            out_specs=pl.BlockSpec((count, 1, 1), lambda i, *_: (0, 0, 0)),
            scratch_shapes=[pltpu.VMEM((8, sec_size), jnp.float32)],
        ),
        out_shape=jax.ShapeDtypeStruct((count, 1, 1), jnp.float32),
    )(block_index.reshape(1), left_live, right_live, state)


def row_major(array):
    return with_layout_constraint(array, Layout(major_to_minor=tuple(range(array.ndim))))


def small_lookup(table, index):
    return lax.dynamic_index_in_dim(table, index, 0, keepdims=False)


def table_entry(table, row, column):
    return small_lookup(small_lookup(table, row), column)


def per_device(state, left_env, right_env, site_ops, left_live, right_live):
    pairs = site_ops.shape[1]
    sec_size = state.shape[1]
    block_index = lax.axis_index("left") * lax.axis_size("right") + lax.axis_index("right")
    own_pair = block_index % pairs
    sector = block_index // pairs
    steps = (jnp.arange(pairs, dtype=jnp.int32) + 1) // 2
    own_step = small_lookup(steps, own_pair)
    positions = jnp.arange(sec_size, dtype=jnp.int32)
    row_mask = (positions < small_lookup(left_live, sector) * BLOCK).astype(jnp.float32)
    col_mask = (positions < small_lookup(right_live, sector + own_step) * BLOCK).astype(jnp.float32)
    live = row_mask[:, None] * col_mask[None, :]
    entries = float(state.shape[0] * sec_size * sec_size * lax.axis_size(AXES))

    masked = state[0] * live
    start_sum = exchange_sum(
        masked_square_sum(pairs, block_index.astype(jnp.int32), left_live, right_live, state)
    )[0, 0]
    start_mean = start_sum / entries
    scale = jnp.sqrt(start_mean + 1e-06)
    vector = lax.optimization_barrier(masked / scale)
    rows = sec_size // CHUNKS
    pieces = [
        row_major((masked[c * rows:(c + 1) * rows] / scale).astype(jnp.bfloat16))
        for c in range(CHUNKS)
    ]
    rounded = jnp.concatenate(pieces, axis=0)

    weights = []
    for offset in (2, 3):
        source_pair = (own_pair - offset) % pairs
        valid = block_index >= offset
        weights.append(
            jnp.where(
                valid, table_entry(site_ops[0], own_pair, source_pair), jnp.zeros((), jnp.float32)
            )
        )

    part_one = jnp.dot(rounded, right_env[1, 0], preferred_element_type=jnp.float32).astype(
        jnp.bfloat16
    )
    diag_weight = table_entry(site_ops[1], own_pair, own_pair)
    image_one = diag_weight * jnp.dot(left_env[1, 0], part_one, preferred_element_type=jnp.float32)

    image_one, pieces[-1] = lax.optimization_barrier((image_one, pieces[-1]))
    parts = []
    for c in range(CHUNKS):
        far_two = shift_up(pieces[c], 2)
        far_three = shift_up(far_two, 1)
        source = (
            weights[0] * far_two.astype(jnp.float32) + weights[1] * far_three.astype(jnp.float32)
        ).astype(jnp.bfloat16)
        parts.append(
            jnp.dot(source, right_env[0, 0], preferred_element_type=jnp.float32).astype(jnp.bfloat16)
        )
    part_zero = jnp.concatenate(parts, axis=0)
    image = jnp.dot(left_env[0, 0], part_zero, preferred_element_type=jnp.float32) + image_one
    image = row_major(image * live)

    sums = all_sum(jnp.sum(jnp.stack([vector * image, image * image]), axis=(1, 2)))
    vector_mean = start_mean / (start_mean + 1e-06)
    means = sums / entries
    swapped = means[::-1]
    lane = lax.broadcasted_iota(jnp.int32, means.shape, 0)
    coefficients = jnp.where(
        lane == 0, means, jnp.sqrt(means - swapped * swapped * (2.0 - vector_mean) + 1e-06)
    )
    residual = image - coefficients[0] * vector
    next_vector = residual * (1.0 / coefficients[1])
    return (next_vector[None], coefficients)


def solution(mesh):
    in_specs = (
        P(AXES, None, None),
        P(None, AXES, None, None),
        P(None, AXES, None, None),
        P(),
        P(),
        P(),
    )
    out_specs = (P(AXES, None, None), P())
    return jax.shard_map(
        per_device, mesh=mesh, in_specs=in_specs, out_specs=out_specs, check_vma=False
    )
```

```python
import functools

import jax
import jax.numpy as jnp
from jax import lax
from jax.sharding import PartitionSpec as P
from jax.experimental.layout import Layout, with_layout_constraint
from jax.experimental import pallas as pl
from jax.experimental.pallas import tpu as pltpu

BLOCK = 256
AXES = ("left", "right")
CHUNKS = 4


def shift_up(block, distance):
    devices = range(lax.axis_size(AXES))
    route = [(i - distance, i) for i in devices if i - distance in devices]
    return lax.ppermute(block, AXES, route)


def all_sum(values):
    count = lax.axis_size(AXES)
    return exchange_sum(jnp.broadcast_to(values[None], (count,) + values.shape))


def exchange_sum(spread):
    return jnp.sum(lax.all_to_all(spread, AXES, 0, 0, tiled=True), axis=0)


def square_sum_kernel(pairs, index_ref, left_ref, right_ref, state_ref, out_ref, acc_ref):
    step = pl.program_id(0)
    rows, cols = state_ref.shape[1], state_ref.shape[2]
    sector = index_ref[0] // pairs
    pair = index_ref[0] % pairs
    row_limit = left_ref[sector] * BLOCK
    col_limit = right_ref[sector + (pair + 1) // 2] * BLOCK

    @pl.when(step == 0)
    def _():
        acc_ref[...] = jnp.zeros_like(acc_ref)

    @pl.when(step * rows < row_limit)
    def _():
        x = state_ref[0]
        col_ids = lax.broadcasted_iota(jnp.int32, (rows, cols), 1)
        x = jnp.where(col_ids < col_limit, x, 0.0)
        acc_ref[...] += jnp.sum((x * x).reshape(rows // 8, 8, cols), axis=0)

    @pl.when(step == pl.num_programs(0) - 1)
    def _():
        out_ref[...] = jnp.full(out_ref.shape, jnp.sum(acc_ref[...]), jnp.float32)


def masked_square_sum(pairs, block_index, left_live, right_live, state):
    count = lax.axis_size(AXES)
    sec_size = state.shape[1]
    rows = 256
    return pl.pallas_call(
        functools.partial(square_sum_kernel, pairs),
        grid_spec=pltpu.PrefetchScalarGridSpec(
            num_scalar_prefetch=3,
            grid=(sec_size // rows,),
            in_specs=[pl.BlockSpec((1, rows, sec_size), lambda i, *_: (0, i, 0))],
            out_specs=pl.BlockSpec((count, 1, 1), lambda i, *_: (0, 0, 0)),
            scratch_shapes=[pltpu.VMEM((8, sec_size), jnp.float32)],
        ),
        out_shape=jax.ShapeDtypeStruct((count, 1, 1), jnp.float32),
    )(block_index.reshape(1), left_live, right_live, state)


def row_major(array):
    return with_layout_constraint(array, Layout(major_to_minor=tuple(range(array.ndim))))


def small_lookup(table, index):
    return lax.dynamic_index_in_dim(table, index, 0, keepdims=False)


def table_entry(table, row, column):
    return small_lookup(small_lookup(table, row), column)


def per_device(state, left_env, right_env, site_ops, left_live, right_live):
    pairs = site_ops.shape[1]
    sec_size = state.shape[1]
    block_index = lax.axis_index("left") * lax.axis_size("right") + lax.axis_index("right")
    own_pair = block_index % pairs
    sector = block_index // pairs
    steps = (jnp.arange(pairs, dtype=jnp.int32) + 1) // 2
    own_step = small_lookup(steps, own_pair)
    positions = jnp.arange(sec_size, dtype=jnp.int32)
    row_mask = (positions < small_lookup(left_live, sector) * BLOCK).astype(jnp.float32)
    col_mask = (positions < small_lookup(right_live, sector + own_step) * BLOCK).astype(jnp.float32)
    live = row_mask[:, None] * col_mask[None, :]
    entries = float(state.shape[0] * sec_size * sec_size * lax.axis_size(AXES))

    masked = state[0] * live
    start_sum = exchange_sum(
        masked_square_sum(pairs, block_index.astype(jnp.int32), left_live, right_live, state)
    )[0, 0]
    start_mean = start_sum / entries
    scale = jnp.sqrt(start_mean + 1e-06)
    vector = masked / scale
    rows = sec_size // CHUNKS
    pieces = [
        row_major((masked[c * rows:(c + 1) * rows] / scale).astype(jnp.bfloat16))
        for c in range(CHUNKS)
    ]
    rounded = jnp.concatenate(pieces, axis=0)

    weights = []
    for offset in (2, 3):
        source_pair = (own_pair - offset) % pairs
        valid = block_index >= offset
        weights.append(
            jnp.where(
                valid, table_entry(site_ops[0], own_pair, source_pair), jnp.zeros((), jnp.float32)
            )
        )

    part_one = jnp.dot(rounded, right_env[1, 0], preferred_element_type=jnp.float32).astype(
        jnp.bfloat16
    )
    diag_weight = table_entry(site_ops[1], own_pair, own_pair)
    image_one = diag_weight * jnp.dot(left_env[1, 0], part_one, preferred_element_type=jnp.float32)

    image_one, pieces[-1] = lax.optimization_barrier((image_one, pieces[-1]))
    parts = []
    for c in range(CHUNKS):
        far_two = shift_up(pieces[c], 2)
        far_three = shift_up(far_two, 1)
        source = (
            weights[0] * far_two.astype(jnp.float32) + weights[1] * far_three.astype(jnp.float32)
        ).astype(jnp.bfloat16)
        parts.append(
            jnp.dot(source, right_env[0, 0], preferred_element_type=jnp.float32).astype(jnp.bfloat16)
        )
    part_zero = jnp.concatenate(parts, axis=0)
    image = jnp.dot(left_env[0, 0], part_zero, preferred_element_type=jnp.float32) + image_one
    image = row_major(image * live)

    sums = all_sum(jnp.sum(jnp.stack([vector * image, image * image]), axis=(1, 2)))
    vector_mean = start_mean / (start_mean + 1e-06)
    means = sums / entries
    swapped = means[::-1]
    lane = lax.broadcasted_iota(jnp.int32, means.shape, 0)
    coefficients = jnp.where(
        lane == 0, means, jnp.sqrt(means - swapped * swapped * (2.0 - vector_mean) + 1e-06)
    )
    residual = image - coefficients[0] * vector
    next_vector = residual / coefficients[1]
    return (next_vector[None], coefficients)


def solution(mesh):
    in_specs = (
        P(AXES, None, None),
        P(None, AXES, None, None),
        P(None, AXES, None, None),
        P(),
        P(),
        P(),
    )
    out_specs = (P(AXES, None, None), P())
    return jax.shard_map(
        per_device, mesh=mesh, in_specs=in_specs, out_specs=out_specs, check_vma=False
    )
```

```python
import functools

import jax
import jax.numpy as jnp
from jax import lax
from jax.sharding import PartitionSpec as P
from jax.experimental.layout import Layout, with_layout_constraint
from jax.experimental import pallas as pl
from jax.experimental.pallas import tpu as pltpu

BLOCK = 256
AXES = ("left", "right")
CHUNKS = 4


def shift_up(block, distance):
    devices = range(lax.axis_size(AXES))
    route = [(i - distance, i) for i in devices if i - distance in devices]
    return lax.ppermute(block, AXES, route)


def all_sum(values):
    count = lax.axis_size(AXES)
    return exchange_sum(jnp.broadcast_to(values[None], (count,) + values.shape))


def exchange_sum(spread):
    return jnp.sum(lax.all_to_all(spread, AXES, 0, 0, tiled=True), axis=0)


def square_sum_kernel(pairs, index_ref, left_ref, right_ref, state_ref, out_ref, acc_ref):
    step = pl.program_id(0)
    rows, cols = state_ref.shape[1], state_ref.shape[2]
    sector = index_ref[0] // pairs
    pair = index_ref[0] % pairs
    row_limit = left_ref[sector] * BLOCK
    col_limit = right_ref[sector + (pair + 1) // 2] * BLOCK

    @pl.when(step == 0)
    def _():
        acc_ref[...] = jnp.zeros_like(acc_ref)

    @pl.when(step * rows < row_limit)
    def _():
        x = state_ref[0]
        col_ids = lax.broadcasted_iota(jnp.int32, (rows, cols), 1)
        x = jnp.where(col_ids < col_limit, x, 0.0)
        acc_ref[...] += jnp.sum((x * x).reshape(rows // 8, 8, cols), axis=0)

    @pl.when(step == pl.num_programs(0) - 1)
    def _():
        out_ref[...] = jnp.full(out_ref.shape, jnp.sum(acc_ref[...]), jnp.float32)


def masked_square_sum(pairs, block_index, left_live, right_live, state):
    count = lax.axis_size(AXES)
    sec_size = state.shape[1]
    rows = BLOCK // 2
    return pl.pallas_call(
        functools.partial(square_sum_kernel, pairs),
        grid_spec=pltpu.PrefetchScalarGridSpec(
            num_scalar_prefetch=3,
            grid=(sec_size // rows,),
            in_specs=[pl.BlockSpec((1, rows, sec_size), lambda i, *_: (0, i, 0))],
            out_specs=pl.BlockSpec((count, 1, 1), lambda i, *_: (0, 0, 0)),
            scratch_shapes=[pltpu.VMEM((8, sec_size), jnp.float32)],
        ),
        out_shape=jax.ShapeDtypeStruct((count, 1, 1), jnp.float32),
    )(block_index.reshape(1), left_live, right_live, state)


def row_major(array):
    return with_layout_constraint(array, Layout(major_to_minor=tuple(range(array.ndim))))


def small_lookup(table, index):
    return lax.dynamic_index_in_dim(table, index, 0, keepdims=False)


def table_entry(table, row, column):
    return small_lookup(small_lookup(table, row), column)


def per_device(state, left_env, right_env, site_ops, left_live, right_live):
    pairs = site_ops.shape[1]
    sec_size = state.shape[1]
    block_index = lax.axis_index("left") * lax.axis_size("right") + lax.axis_index("right")
    own_pair = block_index % pairs
    sector = block_index // pairs
    steps = (jnp.arange(pairs, dtype=jnp.int32) + 1) // 2
    own_step = small_lookup(steps, own_pair)
    positions = jnp.arange(sec_size, dtype=jnp.int32)
    row_mask = (positions < small_lookup(left_live, sector) * BLOCK).astype(jnp.float32)
    col_mask = (positions < small_lookup(right_live, sector + own_step) * BLOCK).astype(jnp.float32)
    live = row_mask[:, None] * col_mask[None, :]
    entries = float(state.shape[0] * sec_size * sec_size * lax.axis_size(AXES))

    masked = state[0] * live
    start_sum = exchange_sum(
        masked_square_sum(pairs, block_index.astype(jnp.int32), left_live, right_live, state)
    )[0, 0]
    start_mean = start_sum / entries
    scale = jnp.sqrt(start_mean + 1e-06)
    vector = masked / scale
    rows = sec_size // CHUNKS
    pieces = [
        row_major((masked[c * rows:(c + 1) * rows] / scale).astype(jnp.bfloat16))
        for c in range(CHUNKS)
    ]
    rounded = jnp.concatenate(pieces, axis=0)

    weights = []
    for offset in (2, 3):
        source_pair = (own_pair - offset) % pairs
        valid = block_index >= offset
        weights.append(
            jnp.where(
                valid, table_entry(site_ops[0], own_pair, source_pair), jnp.zeros((), jnp.float32)
            )
        )

    part_one = jnp.dot(rounded, right_env[1, 0], preferred_element_type=jnp.float32).astype(
        jnp.bfloat16
    )
    diag_weight = table_entry(site_ops[1], own_pair, own_pair)
    image_one = diag_weight * jnp.dot(left_env[1, 0], part_one, preferred_element_type=jnp.float32)

    image_one, pieces[-1] = lax.optimization_barrier((image_one, pieces[-1]))
    parts = []
    for c in range(CHUNKS):
        far_two = shift_up(pieces[c], 2)
        far_three = shift_up(far_two, 1)
        source = (
            weights[0] * far_two.astype(jnp.float32) + weights[1] * far_three.astype(jnp.float32)
        ).astype(jnp.bfloat16)
        parts.append(
            jnp.dot(source, right_env[0, 0], preferred_element_type=jnp.float32).astype(jnp.bfloat16)
        )
    part_zero = jnp.concatenate(parts, axis=0)
    image = jnp.dot(left_env[0, 0], part_zero, preferred_element_type=jnp.float32) + image_one
    image = row_major(image * live)

    sums = all_sum(jnp.sum(jnp.stack([vector * image, image * image]), axis=(1, 2)))
    vector_mean = start_mean / (start_mean + 1e-06)
    means = sums / entries
    swapped = means[::-1]
    lane = lax.broadcasted_iota(jnp.int32, means.shape, 0)
    coefficients = jnp.where(
        lane == 0, means, jnp.sqrt(means - swapped * swapped * (2.0 - vector_mean) + 1e-06)
    )
    residual = image - coefficients[0] * vector
    next_vector = residual / coefficients[1]
    return (next_vector[None], coefficients)


def solution(mesh):
    in_specs = (
        P(AXES, None, None),
        P(None, AXES, None, None),
        P(None, AXES, None, None),
        P(),
        P(),
        P(),
    )
    out_specs = (P(AXES, None, None), P())
    return jax.shard_map(
        per_device, mesh=mesh, in_specs=in_specs, out_specs=out_specs, check_vma=False
    )
```

```python
import functools

import jax
import jax.numpy as jnp
from jax import lax
from jax.sharding import PartitionSpec as P
from jax.experimental.layout import Layout, with_layout_constraint
from jax.experimental import pallas as pl
from jax.experimental.pallas import tpu as pltpu

BLOCK = 256
AXES = ("left", "right")
CHUNKS = 4


def shift_up(block, distance):
    devices = range(lax.axis_size(AXES))
    route = [(i - distance, i) for i in devices if i - distance in devices]
    return lax.ppermute(block, AXES, route)


def all_sum(values):
    count = lax.axis_size(AXES)
    return exchange_sum(jnp.broadcast_to(values[None], (count,) + values.shape))


def exchange_sum(spread):
    return jnp.sum(lax.all_to_all(spread, AXES, 0, 0, tiled=True), axis=0)


def square_sum_kernel(pairs, index_ref, left_ref, right_ref, state_ref, out_ref, acc_ref):
    step = pl.program_id(0)
    rows, cols = state_ref.shape[1], state_ref.shape[2]
    sector = index_ref[0] // pairs
    pair = index_ref[0] % pairs
    row_limit = left_ref[sector] * BLOCK
    col_limit = right_ref[sector + (pair + 1) // 2] * BLOCK

    @pl.when(step == 0)
    def _():
        acc_ref[...] = jnp.zeros_like(acc_ref)

    @pl.when(step * rows < row_limit)
    def _():
        x = state_ref[0]
        row_ids = step * rows + lax.broadcasted_iota(jnp.int32, (rows, cols), 0)
        col_ids = lax.broadcasted_iota(jnp.int32, (rows, cols), 1)
        x = jnp.where((row_ids < row_limit) & (col_ids < col_limit), x, 0.0)
        acc_ref[...] += jnp.sum((x * x).reshape(rows // 8, 8, cols), axis=0)

    @pl.when(step == pl.num_programs(0) - 1)
    def _():
        out_ref[...] = jnp.full(out_ref.shape, jnp.sum(acc_ref[...]), jnp.float32)


def masked_square_sum(pairs, block_index, left_live, right_live, state):
    count = lax.axis_size(AXES)
    sec_size = state.shape[1]
    rows = 2 * BLOCK
    return pl.pallas_call(
        functools.partial(square_sum_kernel, pairs),
        grid_spec=pltpu.PrefetchScalarGridSpec(
            num_scalar_prefetch=3,
            grid=(sec_size // rows,),
            in_specs=[pl.BlockSpec((1, rows, sec_size), lambda i, *_: (0, i, 0))],
            out_specs=pl.BlockSpec((count, 1, 1), lambda i, *_: (0, 0, 0)),
            scratch_shapes=[pltpu.VMEM((8, sec_size), jnp.float32)],
        ),
        out_shape=jax.ShapeDtypeStruct((count, 1, 1), jnp.float32),
    )(block_index.reshape(1), left_live, right_live, state)


def row_major(array):
    return with_layout_constraint(array, Layout(major_to_minor=tuple(range(array.ndim))))


def small_lookup(table, index):
    return lax.dynamic_index_in_dim(table, index, 0, keepdims=False)


def table_entry(table, row, column):
    return small_lookup(small_lookup(table, row), column)


def per_device(state, left_env, right_env, site_ops, left_live, right_live):
    pairs = site_ops.shape[1]
    sec_size = state.shape[1]
    block_index = lax.axis_index("left") * lax.axis_size("right") + lax.axis_index("right")
    own_pair = block_index % pairs
    sector = block_index // pairs
    steps = (jnp.arange(pairs, dtype=jnp.int32) + 1) // 2
    own_step = small_lookup(steps, own_pair)
    positions = jnp.arange(sec_size, dtype=jnp.int32)
    row_mask = (positions < small_lookup(left_live, sector) * BLOCK).astype(jnp.float32)
    col_mask = (positions < small_lookup(right_live, sector + own_step) * BLOCK).astype(jnp.float32)
    live = row_mask[:, None] * col_mask[None, :]
    entries = float(state.shape[0] * sec_size * sec_size * lax.axis_size(AXES))

    masked = state[0] * live
    start_sum = exchange_sum(
        masked_square_sum(pairs, block_index.astype(jnp.int32), left_live, right_live, state)
    )[0, 0]
    start_mean = start_sum / entries
    scale = jnp.sqrt(start_mean + 1e-06)
    vector = masked / scale
    rows = sec_size // CHUNKS
    pieces = [
        row_major((masked[c * rows:(c + 1) * rows] / scale).astype(jnp.bfloat16))
        for c in range(CHUNKS)
    ]
    rounded = jnp.concatenate(pieces, axis=0)

    weights = []
    for offset in (2, 3):
        source_pair = (own_pair - offset) % pairs
        valid = block_index >= offset
        weights.append(
            jnp.where(
                valid, table_entry(site_ops[0], own_pair, source_pair), jnp.zeros((), jnp.float32)
            )
        )

    part_one = jnp.dot(rounded, right_env[1, 0], preferred_element_type=jnp.float32).astype(
        jnp.bfloat16
    )
    diag_weight = table_entry(site_ops[1], own_pair, own_pair)
    image_one = diag_weight * jnp.dot(left_env[1, 0], part_one, preferred_element_type=jnp.float32)

    image_one, pieces[-1] = lax.optimization_barrier((image_one, pieces[-1]))
    parts = []
    for c in range(CHUNKS):
        far_two = shift_up(pieces[c], 2)
        far_three = shift_up(far_two, 1)
        source = (
            weights[0] * far_two.astype(jnp.float32) + weights[1] * far_three.astype(jnp.float32)
        ).astype(jnp.bfloat16)
        parts.append(
            jnp.dot(source, right_env[0, 0], preferred_element_type=jnp.float32).astype(jnp.bfloat16)
        )
    part_zero = jnp.concatenate(parts, axis=0)
    image = jnp.dot(left_env[0, 0], part_zero, preferred_element_type=jnp.float32) + image_one
    image = row_major(image * live)

    sums = all_sum(jnp.sum(jnp.stack([vector * image, image * image]), axis=(1, 2)))
    vector_mean = start_mean / (start_mean + 1e-06)
    means = sums / entries
    swapped = means[::-1]
    lane = lax.broadcasted_iota(jnp.int32, means.shape, 0)
    coefficients = jnp.where(
        lane == 0, means, jnp.sqrt(means - swapped * swapped * (2.0 - vector_mean) + 1e-06)
    )
    residual = image - coefficients[0] * vector
    next_vector = residual / coefficients[1]
    return (next_vector[None], coefficients)


def solution(mesh):
    in_specs = (
        P(AXES, None, None),
        P(None, AXES, None, None),
        P(None, AXES, None, None),
        P(),
        P(),
        P(),
    )
    out_specs = (P(AXES, None, None), P())
    return jax.shard_map(
        per_device, mesh=mesh, in_specs=in_specs, out_specs=out_specs, check_vma=False
    )
```

```python
import functools

import jax
import jax.numpy as jnp
from jax import lax
from jax.sharding import PartitionSpec as P
from jax.experimental.layout import Layout, with_layout_constraint
from jax.experimental import pallas as pl
from jax.experimental.pallas import tpu as pltpu

BLOCK = 256
AXES = ("left", "right")
CHUNKS = 4


def shift_up(block, distance):
    devices = range(lax.axis_size(AXES))
    route = [(i - distance, i) for i in devices if i - distance in devices]
    return lax.ppermute(block, AXES, route)


def all_sum(values):
    count = lax.axis_size(AXES)
    return exchange_sum(jnp.broadcast_to(values[None], (count,) + values.shape))


def exchange_sum(spread):
    return jnp.sum(lax.all_to_all(spread, AXES, 0, 0, tiled=True), axis=0)


def square_sum_kernel(pairs, index_ref, left_ref, right_ref, state_ref, out_ref, acc_ref):
    step = pl.program_id(0)
    rows, cols = state_ref.shape[1], state_ref.shape[2]
    sector = index_ref[0] // pairs
    pair = index_ref[0] % pairs
    row_limit = left_ref[sector] * BLOCK
    col_limit = right_ref[sector + (pair + 1) // 2] * BLOCK

    @pl.when(step == 0)
    def _():
        acc_ref[...] = jnp.zeros_like(acc_ref)

    @pl.when(step * rows < row_limit)
    def _():
        x = state_ref[0]
        row_live = step * rows + lax.broadcasted_iota(jnp.int32, (rows, 1), 0) < row_limit
        col_live = lax.broadcasted_iota(jnp.int32, (1, cols), 1) < col_limit
        x = jnp.where(row_live & col_live, x, 0.0)
        acc_ref[...] += jnp.sum((x * x).reshape(rows // 8, 8, cols), axis=0)

    @pl.when(step == pl.num_programs(0) - 1)
    def _():
        out_ref[...] = jnp.full(out_ref.shape, jnp.sum(acc_ref[...]), jnp.float32)


def masked_square_sum(pairs, block_index, left_live, right_live, state):
    count = lax.axis_size(AXES)
    sec_size = state.shape[1]
    rows = 2 * BLOCK
    return pl.pallas_call(
        functools.partial(square_sum_kernel, pairs),
        grid_spec=pltpu.PrefetchScalarGridSpec(
            num_scalar_prefetch=3,
            grid=(sec_size // rows,),
            in_specs=[pl.BlockSpec((1, rows, sec_size), lambda i, *_: (0, i, 0))],
            out_specs=pl.BlockSpec((count, 1, 1), lambda i, *_: (0, 0, 0)),
            scratch_shapes=[pltpu.VMEM((8, sec_size), jnp.float32)],
        ),
        out_shape=jax.ShapeDtypeStruct((count, 1, 1), jnp.float32),
    )(block_index.reshape(1), left_live, right_live, state)


def row_major(array):
    return with_layout_constraint(array, Layout(major_to_minor=tuple(range(array.ndim))))


def small_lookup(table, index):
    return lax.dynamic_index_in_dim(table, index, 0, keepdims=False)


def table_entry(table, row, column):
    return small_lookup(small_lookup(table, row), column)


def per_device(state, left_env, right_env, site_ops, left_live, right_live):
    pairs = site_ops.shape[1]
    sec_size = state.shape[1]
    block_index = lax.axis_index("left") * lax.axis_size("right") + lax.axis_index("right")
    own_pair = block_index % pairs
    sector = block_index // pairs
    steps = (jnp.arange(pairs, dtype=jnp.int32) + 1) // 2
    own_step = small_lookup(steps, own_pair)
    positions = jnp.arange(sec_size, dtype=jnp.int32)
    row_mask = (positions < small_lookup(left_live, sector) * BLOCK).astype(jnp.float32)
    col_mask = (positions < small_lookup(right_live, sector + own_step) * BLOCK).astype(jnp.float32)
    live = row_mask[:, None] * col_mask[None, :]
    entries = float(state.shape[0] * sec_size * sec_size * lax.axis_size(AXES))

    masked = state[0] * live
    start_sum = exchange_sum(
        masked_square_sum(pairs, block_index.astype(jnp.int32), left_live, right_live, state)
    )[0, 0]
    start_mean = start_sum / entries
    scale = jnp.sqrt(start_mean + 1e-06)
    vector = masked / scale
    rows = sec_size // CHUNKS
    pieces = [
        row_major((masked[c * rows:(c + 1) * rows] / scale).astype(jnp.bfloat16))
        for c in range(CHUNKS)
    ]
    rounded = jnp.concatenate(pieces, axis=0)

    weights = []
    for offset in (2, 3):
        source_pair = (own_pair - offset) % pairs
        valid = block_index >= offset
        weights.append(
            jnp.where(
                valid, table_entry(site_ops[0], own_pair, source_pair), jnp.zeros((), jnp.float32)
            )
        )

    part_one = jnp.dot(rounded, right_env[1, 0], preferred_element_type=jnp.float32).astype(
        jnp.bfloat16
    )
    diag_weight = table_entry(site_ops[1], own_pair, own_pair)
    image_one = diag_weight * jnp.dot(left_env[1, 0], part_one, preferred_element_type=jnp.float32)

    image_one, pieces[-1] = lax.optimization_barrier((image_one, pieces[-1]))
    parts = []
    for c in range(CHUNKS):
        far_two = shift_up(pieces[c], 2)
        far_three = shift_up(far_two, 1)
        source = (
            weights[0] * far_two.astype(jnp.float32) + weights[1] * far_three.astype(jnp.float32)
        ).astype(jnp.bfloat16)
        parts.append(
            jnp.dot(source, right_env[0, 0], preferred_element_type=jnp.float32).astype(jnp.bfloat16)
        )
    part_zero = jnp.concatenate(parts, axis=0)
    image = jnp.dot(left_env[0, 0], part_zero, preferred_element_type=jnp.float32) + image_one
    image = row_major(image * live)

    sums = all_sum(jnp.sum(jnp.stack([vector * image, image * image]), axis=(1, 2)))
    vector_mean = start_mean / (start_mean + 1e-06)
    means = sums / entries
    swapped = means[::-1]
    lane = lax.broadcasted_iota(jnp.int32, means.shape, 0)
    coefficients = jnp.where(
        lane == 0, means, jnp.sqrt(means - swapped * swapped * (2.0 - vector_mean) + 1e-06)
    )
    residual = image - coefficients[0] * vector
    next_vector = residual / coefficients[1]
    return (next_vector[None], coefficients)


def solution(mesh):
    in_specs = (
        P(AXES, None, None),
        P(None, AXES, None, None),
        P(None, AXES, None, None),
        P(),
        P(),
        P(),
    )
    out_specs = (P(AXES, None, None), P())
    return jax.shard_map(
        per_device, mesh=mesh, in_specs=in_specs, out_specs=out_specs, check_vma=False
    )
```

```python
import functools

import jax
import jax.numpy as jnp
from jax import lax
from jax.sharding import PartitionSpec as P
from jax.experimental.layout import Layout, with_layout_constraint
from jax.experimental import pallas as pl
from jax.experimental.pallas import tpu as pltpu

BLOCK = 256
AXES = ("left", "right")
CHUNKS = 4


def shift_up(block, distance):
    devices = range(lax.axis_size(AXES))
    route = [(i - distance, i) for i in devices if i - distance in devices]
    return lax.ppermute(block, AXES, route)


def all_sum(values):
    count = lax.axis_size(AXES)
    return exchange_sum(jnp.broadcast_to(values[None], (count,) + values.shape))


def exchange_sum(spread):
    return jnp.sum(lax.all_to_all(spread, AXES, 0, 0, tiled=True), axis=0)


def square_sum_kernel(pairs, index_ref, left_ref, right_ref, state_ref, out_ref, acc_ref):
    step = pl.program_id(0)
    rows, cols = state_ref.shape[1], state_ref.shape[2]
    sector = index_ref[0] // pairs
    pair = index_ref[0] % pairs
    row_limit = left_ref[sector] * BLOCK
    col_limit = right_ref[sector + (pair + 1) // 2] * BLOCK

    @pl.when(step == 0)
    def _():
        acc_ref[...] = jnp.zeros_like(acc_ref)

    @pl.when(step * rows < row_limit)
    def _():
        x = state_ref[0]
        row_live = step * rows + lax.broadcasted_iota(jnp.int32, (rows, 1), 0) < row_limit
        col_live = lax.broadcasted_iota(jnp.int32, (1, cols), 1) < col_limit
        x = jnp.where(row_live & col_live, x, 0.0)
        acc_ref[...] += jnp.sum((x * x).reshape(rows // 8, 8, cols), axis=0)

    @pl.when(step == pl.num_programs(0) - 1)
    def _():
        out_ref[...] = jnp.full(out_ref.shape, jnp.sum(acc_ref[...]), jnp.float32)


def masked_square_sum(pairs, block_index, left_live, right_live, state):
    count = lax.axis_size(AXES)
    sec_size = state.shape[1]
    rows = 4 * BLOCK
    return pl.pallas_call(
        functools.partial(square_sum_kernel, pairs),
        grid_spec=pltpu.PrefetchScalarGridSpec(
            num_scalar_prefetch=3,
            grid=(sec_size // rows,),
            in_specs=[pl.BlockSpec((1, rows, sec_size), lambda i, *_: (0, i, 0))],
            out_specs=pl.BlockSpec((count, 1, 1), lambda i, *_: (0, 0, 0)),
            scratch_shapes=[pltpu.VMEM((8, sec_size), jnp.float32)],
        ),
        out_shape=jax.ShapeDtypeStruct((count, 1, 1), jnp.float32),
    )(block_index.reshape(1), left_live, right_live, state)


def row_major(array):
    return with_layout_constraint(array, Layout(major_to_minor=tuple(range(array.ndim))))


def small_lookup(table, index):
    return lax.dynamic_index_in_dim(table, index, 0, keepdims=False)


def table_entry(table, row, column):
    return small_lookup(small_lookup(table, row), column)


def per_device(state, left_env, right_env, site_ops, left_live, right_live):
    pairs = site_ops.shape[1]
    sec_size = state.shape[1]
    block_index = lax.axis_index("left") * lax.axis_size("right") + lax.axis_index("right")
    own_pair = block_index % pairs
    sector = block_index // pairs
    steps = (jnp.arange(pairs, dtype=jnp.int32) + 1) // 2
    own_step = small_lookup(steps, own_pair)
    positions = jnp.arange(sec_size, dtype=jnp.int32)
    row_mask = (positions < small_lookup(left_live, sector) * BLOCK).astype(jnp.float32)
    col_mask = (positions < small_lookup(right_live, sector + own_step) * BLOCK).astype(jnp.float32)
    live = row_mask[:, None] * col_mask[None, :]
    entries = float(state.shape[0] * sec_size * sec_size * lax.axis_size(AXES))

    masked = state[0] * live
    start_sum = exchange_sum(
        masked_square_sum(pairs, block_index.astype(jnp.int32), left_live, right_live, state)
    )[0, 0]
    start_mean = start_sum / entries
    scale = jnp.sqrt(start_mean + 1e-06)
    vector = masked / scale
    rows = sec_size // CHUNKS
    pieces = [
        row_major((masked[c * rows:(c + 1) * rows] / scale).astype(jnp.bfloat16))
        for c in range(CHUNKS)
    ]
    rounded = jnp.concatenate(pieces, axis=0)

    weights = []
    for offset in (2, 3):
        source_pair = (own_pair - offset) % pairs
        valid = block_index >= offset
        weights.append(
            jnp.where(
                valid, table_entry(site_ops[0], own_pair, source_pair), jnp.zeros((), jnp.float32)
            )
        )

    part_one = jnp.dot(rounded, right_env[1, 0], preferred_element_type=jnp.float32).astype(
        jnp.bfloat16
    )
    diag_weight = table_entry(site_ops[1], own_pair, own_pair)
    image_one = diag_weight * jnp.dot(left_env[1, 0], part_one, preferred_element_type=jnp.float32)

    image_one, pieces[-1] = lax.optimization_barrier((image_one, pieces[-1]))
    parts = []
    for c in range(CHUNKS):
        far_two = shift_up(pieces[c], 2)
        far_three = shift_up(far_two, 1)
        source = (
            weights[0] * far_two.astype(jnp.float32) + weights[1] * far_three.astype(jnp.float32)
        ).astype(jnp.bfloat16)
        parts.append(
            jnp.dot(source, right_env[0, 0], preferred_element_type=jnp.float32).astype(jnp.bfloat16)
        )
    part_zero = jnp.concatenate(parts, axis=0)
    image = jnp.dot(left_env[0, 0], part_zero, preferred_element_type=jnp.float32) + image_one
    image = row_major(image * live)

    sums = all_sum(jnp.sum(jnp.stack([vector * image, image * image]), axis=(1, 2)))
    vector_mean = start_mean / (start_mean + 1e-06)
    means = sums / entries
    swapped = means[::-1]
    lane = lax.broadcasted_iota(jnp.int32, means.shape, 0)
    coefficients = jnp.where(
        lane == 0, means, jnp.sqrt(means - swapped * swapped * (2.0 - vector_mean) + 1e-06)
    )
    residual = image - coefficients[0] * vector
    next_vector = residual / coefficients[1]
    return (next_vector[None], coefficients)


def solution(mesh):
    in_specs = (
        P(AXES, None, None),
        P(None, AXES, None, None),
        P(None, AXES, None, None),
        P(),
        P(),
        P(),
    )
    out_specs = (P(AXES, None, None), P())
    return jax.shard_map(
        per_device, mesh=mesh, in_specs=in_specs, out_specs=out_specs, check_vma=False
    )
```

```python
import functools

import jax
import jax.numpy as jnp
from jax import lax
from jax.sharding import PartitionSpec as P
from jax.experimental.layout import Layout, with_layout_constraint
from jax.experimental import pallas as pl
from jax.experimental.pallas import tpu as pltpu

BLOCK = 256
AXES = ("left", "right")
CHUNKS = 4


def shift_up(block, distance):
    devices = range(lax.axis_size(AXES))
    route = [(i - distance, i) for i in devices if i - distance in devices]
    return lax.ppermute(block, AXES, route)


def all_sum(values):
    count = lax.axis_size(AXES)
    return exchange_sum(jnp.broadcast_to(values[None], (count,) + values.shape))


def exchange_sum(spread):
    return jnp.sum(lax.all_to_all(spread, AXES, 0, 0, tiled=True), axis=0)


def square_sum_kernel(pairs, index_ref, left_ref, right_ref, state_ref, out_ref, acc_ref):
    step = pl.program_id(0)
    rows, cols = state_ref.shape[1], state_ref.shape[2]
    sector = index_ref[0] // pairs
    pair = index_ref[0] % pairs
    row_limit = left_ref[sector] * BLOCK
    col_limit = right_ref[sector + (pair + 1) // 2] * BLOCK

    @pl.when(step == 0)
    def _():
        acc_ref[...] = jnp.zeros_like(acc_ref)

    @pl.when(step * rows < row_limit)
    def _():
        x = state_ref[0]
        row_live = step * rows + lax.broadcasted_iota(jnp.int32, (rows, 1), 0) < row_limit
        col_live = lax.broadcasted_iota(jnp.int32, (1, cols), 1) < col_limit
        x = jnp.where(row_live & col_live, x, 0.0)
        acc_ref[...] += jnp.sum((x * x).reshape(rows // 8, 8, cols), axis=0)

    @pl.when(step == pl.num_programs(0) - 1)
    def _():
        out_ref[...] = jnp.full(out_ref.shape, jnp.sum(acc_ref[...]), jnp.float32)


def masked_square_sum(pairs, block_index, left_live, right_live, state):
    count = lax.axis_size(AXES)
    sec_size = state.shape[1]
    rows = 2 * BLOCK
    return pl.pallas_call(
        functools.partial(square_sum_kernel, pairs),
        grid_spec=pltpu.PrefetchScalarGridSpec(
            num_scalar_prefetch=3,
            grid=(sec_size // rows,),
            in_specs=[pl.BlockSpec((1, rows, sec_size), lambda i, *_: (0, i, 0))],
            out_specs=pl.BlockSpec((count, 1, 1), lambda i, *_: (0, 0, 0)),
            scratch_shapes=[pltpu.VMEM((8, sec_size), jnp.float32)],
        ),
        out_shape=jax.ShapeDtypeStruct((count, 1, 1), jnp.float32),
    )(block_index.reshape(1), left_live, right_live, state)


def row_major(array):
    return with_layout_constraint(array, Layout(major_to_minor=tuple(range(array.ndim))))


def small_lookup(table, index):
    return lax.dynamic_index_in_dim(table, index, 0, keepdims=False)


def table_entry(table, row, column):
    return small_lookup(small_lookup(table, row), column)


def per_device(state, left_env, right_env, site_ops, left_live, right_live):
    pairs = site_ops.shape[1]
    sec_size = state.shape[1]
    block_index = lax.axis_index("left") * lax.axis_size("right") + lax.axis_index("right")
    own_pair = block_index % pairs
    sector = block_index // pairs
    steps = (jnp.arange(pairs, dtype=jnp.int32) + 1) // 2
    own_step = small_lookup(steps, own_pair)
    positions = jnp.arange(sec_size, dtype=jnp.int32)
    row_mask = (positions < small_lookup(left_live, sector) * BLOCK).astype(jnp.float32)
    col_mask = (positions < small_lookup(right_live, sector + own_step) * BLOCK).astype(jnp.float32)
    live = row_mask[:, None] * col_mask[None, :]
    entries = float(state.shape[0] * sec_size * sec_size * lax.axis_size(AXES))

    masked = state[0] * live
    start_sum = exchange_sum(
        masked_square_sum(pairs, block_index.astype(jnp.int32), left_live, right_live, state)
    )[0, 0]
    start_mean = start_sum / entries
    scale = jnp.sqrt(start_mean + 1e-06)
    vector = masked / scale
    rows = sec_size // CHUNKS
    pieces = [
        row_major((masked[c * rows:(c + 1) * rows] / scale).astype(jnp.bfloat16))
        for c in range(CHUNKS)
    ]
    rounded = jnp.concatenate(pieces, axis=0)

    weights = []
    for offset in (2, 3):
        source_pair = (own_pair - offset) % pairs
        valid = block_index >= offset
        weights.append(
            jnp.where(
                valid, table_entry(site_ops[0], own_pair, source_pair), jnp.zeros((), jnp.float32)
            )
        )

    part_one = jnp.dot(rounded, right_env[1, 0], preferred_element_type=jnp.float32).astype(
        jnp.bfloat16
    )
    diag_weight = table_entry(site_ops[1], own_pair, own_pair)
    image_one = diag_weight * jnp.dot(left_env[1, 0], part_one, preferred_element_type=jnp.float32)

    image_one, pieces[-2] = lax.optimization_barrier((image_one, pieces[-2]))
    parts = []
    for c in range(CHUNKS):
        far_two = shift_up(pieces[c], 2)
        far_three = shift_up(far_two, 1)
        source = (
            weights[0] * far_two.astype(jnp.float32) + weights[1] * far_three.astype(jnp.float32)
        ).astype(jnp.bfloat16)
        parts.append(
            jnp.dot(source, right_env[0, 0], preferred_element_type=jnp.float32).astype(jnp.bfloat16)
        )
    part_zero = jnp.concatenate(parts, axis=0)
    image = jnp.dot(left_env[0, 0], part_zero, preferred_element_type=jnp.float32) + image_one
    image = row_major(image * live)

    sums = all_sum(jnp.sum(jnp.stack([vector * image, image * image]), axis=(1, 2)))
    vector_mean = start_mean / (start_mean + 1e-06)
    means = sums / entries
    swapped = means[::-1]
    lane = lax.broadcasted_iota(jnp.int32, means.shape, 0)
    coefficients = jnp.where(
        lane == 0, means, jnp.sqrt(means - swapped * swapped * (2.0 - vector_mean) + 1e-06)
    )
    residual = image - coefficients[0] * vector
    next_vector = residual / coefficients[1]
    return (next_vector[None], coefficients)


def solution(mesh):
    in_specs = (
        P(AXES, None, None),
        P(None, AXES, None, None),
        P(None, AXES, None, None),
        P(),
        P(),
        P(),
    )
    out_specs = (P(AXES, None, None), P())
    return jax.shard_map(
        per_device, mesh=mesh, in_specs=in_specs, out_specs=out_specs, check_vma=False
    )
```
